512 devices in a mesh: ingest: 8 (over y, core), owner: 64 (over x, z).
Axes of the slice: x: 4, y: 4, z: 16, core: 2. Of those that a mesh axis runs over, the one named last changes fastest.
Arguments:
- frame_rows: bfloat16 [2112, 28, 1024], P('owner', None, 'ingest'), may hold values from -32 to 32
- route_owner: int32 [2112], P('owner'), may hold values from 0 to 63, as said below
- route_slot: int32 [2112], P('owner'), may hold values from 0 to 32, as said below
- frames: int32 [2112], P('owner'), may hold values from 1 to 28, as said below
- kv_cache: bfloat16 [2112, 8, 70, 256], P('owner', 'ingest'), may hold values from -250 to 250
- conv_cache: bfloat16 [2112, 8, 1024], P('owner', None, 'ingest'), may hold values from -5 to 5
- mig_owner: int32 [2048], P('owner'), may hold values from 0 to 63, as said below
- ln1_gain: float32 [1024], replicated, may hold values from 0.1 to 1.9
- w_qkv: bfloat16 [1024, 8, 384], P(None, 'ingest'), may hold values from -0.1875 to 0.1875
- w_out: bfloat16 [1024, 1024], P('ingest'), may hold values from -0.1875 to 0.1875
- ln2_gain: float32 [1024], replicated, may hold values from 0.1 to 1.9
- w_pw1: bfloat16 [1024, 2, 1024], P(None, None, 'ingest'), may hold values from -0.1875 to 0.1875
- dw_weight: bfloat16 [9, 1024], P(None, 'ingest'), may hold values from -2 to 2
- bn_scale: float32 [1024], P('ingest'), may hold values from 0.1 to 1.9
- bn_shift: float32 [1024], P('ingest'), may hold values from -2.5 to 2.5
- w_pw2: bfloat16 [1024, 1024], P('ingest'), may hold values from -0.1875 to 0.1875
Outputs:
- layer_out: bfloat16 [2112, 28, 1024], P('owner', None, 'ingest')
- kv_next: bfloat16 [2112, 8, 70, 256], P('owner', 'ingest')
- conv_next: bfloat16 [2112, 8, 1024], P('owner', None, 'ingest')
The draws below stay inside these ranges and needn't reach their ends.
Inputs may be any that keep to these rules, and one draw needn't show every extreme that they name: `route_owner`: every owner receives exactly 33 utterances. The utterances that one source device along owner (a block of 33 rows in arrival order) sends to one owner number at most 1, and some source device reaches that number. `route_slot`: the utterances sent to one owner have distinct slots. Every owner holds an utterance with 28 new frames. The utterance in old slot 1 + j of an owner moves to slot 1 + j of owner mig_owner; the 32 utterances of one owner go to 32 different other owners, and every owner receives exactly one utterance for each j.
All inputs are finite; a program needn't handle non-finite values.
Results may differ from the reference program's by a relative error of at most 0.01.
Values may be sent and summed in bfloat16 or wider, within the bound.
No kernel may reach another device: no remote copies, remote signals or barrier semaphores. Data moves between devices by JAX's collectives and lax.ppermute only.
A program may use at most 64 MiB of HBM per device.

```python
import math
import jax
import jax.numpy as jnp
from jax import lax

D = 1024
H = 8
HD = 128
KW = 9
L = 70
CH = 14
BLOCKS = 2
S_OWN = 33
KT = 8
MIG = 32
UTTS = 2112
N_INGEST = 8
N_OWNER = 64


def routing_tables(key):
    first_key, second_key, third_key = jax.random.split(jax.random.fold_in(key, 11), 3)
    owner_order = jax.random.permutation(first_key, N_OWNER)
    inverse = jnp.zeros((N_OWNER,), jnp.int32).at[owner_order].set(jnp.arange(N_OWNER, dtype=jnp.int32))
    offsets = jax.random.permutation(second_key, N_OWNER)[jnp.arange(S_OWN) % N_OWNER]
    destination = owner_order[(inverse[:, None] + offsets[None, :]) % N_OWNER]
    slot_tables = jax.vmap(lambda small_key: jax.random.permutation(small_key, S_OWN))(jax.random.split(third_key, N_OWNER))
    slot_of = slot_tables[destination, jnp.arange(S_OWN)[None, :]]
    return (destination.reshape(-1).astype(jnp.int32), slot_of.reshape(-1).astype(jnp.int32))


def draw_route_owner(key, part):
    return routing_tables(key)[0]


def draw_route_slot(key, part):
    return routing_tables(key)[1]


def draw_frames(key, part):
    first_key, second_key = jax.random.split(jax.random.fold_in(key, 5))
    counts = jax.random.randint(first_key, (UTTS,), 1, BLOCKS * CH + 1)
    chosen = jax.random.randint(second_key, (N_OWNER,), 0, S_OWN)
    return counts.at[jnp.arange(N_OWNER) * S_OWN + chosen].set(BLOCKS * CH).astype(jnp.int32)


def draw_mig_owner(key, part):
    first_key, second_key = jax.random.split(jax.random.fold_in(key, 23))
    owner_order = jax.random.permutation(first_key, N_OWNER)
    inverse = jnp.zeros((N_OWNER,), jnp.int32).at[owner_order].set(jnp.arange(N_OWNER, dtype=jnp.int32))
    offsets = jax.random.permutation(second_key, N_OWNER - 1)[:MIG] + 1
    destination = owner_order[(inverse[:, None] + offsets[None, :]) % N_OWNER]
    return destination.reshape(-1).astype(jnp.int32)


def draw_frame_rows(key, part):
    first_key, second_key, third_key = jax.random.split(jax.random.fold_in(key, 31), 3)
    row_scale = jnp.exp(jax.random.uniform(second_key, (UTTS, BLOCKS * CH, 1), jnp.float32, math.log(0.3), math.log(3.0)))
    col_scale = jnp.exp(jax.random.uniform(third_key, (1, 1, D), jnp.float32, math.log(0.3), math.log(3.0)))
    base_draw = jnp.clip(jax.random.normal(first_key, (UTTS, BLOCKS * CH, D), jnp.float32), -3.5, 3.5)
    return (base_draw * row_scale * col_scale).astype(jnp.bfloat16)


def draw_kv_cache(key, part):
    first_key = jax.random.fold_in(jax.random.fold_in(key, 41), 0)
    shape = (UTTS, H, L, 2 * HD)
    return jnp.clip(jax.random.normal(first_key, shape, jnp.float32), -5.0, 5.0).astype(jnp.bfloat16)


def levels(rng, dims, shards, low, high):
    def one(dim, blocks):
        steps = jax.random.uniform(jax.random.fold_in(jax.random.fold_in(rng, 6), dim), (blocks,), jnp.float32, low / len(shards), high / len(shards))
        return jnp.repeat(jnp.exp(steps), dims[dim] // blocks).reshape((-1,) + (1,) * (len(dims) - dim - 1))

    factor_of = one(*shards[0])
    for cut in shards[1:]:
        factor_of = factor_of * one(*cut)
    return factor_of


def scatter_about(rng, dims, scale, reach, cuts=(), kind=jnp.bfloat16):
    entries = scale * jax.random.normal(rng, dims, jnp.float32)
    if cuts:
        entries = entries * levels(rng, dims, cuts, -0.22, 0.18)
    return jnp.clip(entries, -reach, reach).astype(kind)


def setup_inputs(seed: int = 0) -> dict:
    streams_of = jax.random.split(jax.random.key(seed), 17)
    frame_rows = draw_frame_rows(jax.random.fold_in(streams_of[16], 71), 0)
    route_owner = draw_route_owner(jax.random.fold_in(streams_of[16], 71), 0)
    route_slot = draw_route_slot(jax.random.fold_in(streams_of[16], 71), 0)
    frames = draw_frames(jax.random.fold_in(streams_of[16], 71), 0)
    kv_cache = draw_kv_cache(jax.random.fold_in(streams_of[16], 71), 0)
    conv_cache = scatter_about(streams_of[5], (UTTS, KT, D), 1.0, 5.0, ((0, 64), (2, 8)))
    mig_owner = draw_mig_owner(jax.random.fold_in(streams_of[16], 71), 0)
    ln1_gain = jnp.clip(1.0 + 0.18 * jax.random.normal(streams_of[7], (D,), jnp.float32), 0.1, 1.9)
    w_qkv = scatter_about(streams_of[8], (D, H, 3 * HD), D ** -0.5, 0.1875, ((1, 8),))
    w_out = scatter_about(streams_of[9], (D, D), D ** -0.5, 0.1875, ((0, 8),))
    ln2_gain = jnp.clip(1.0 + 0.18 * jax.random.normal(streams_of[10], (D,), jnp.float32), 0.1, 1.9)
    w_pw1 = scatter_about(streams_of[11], (D, 2, D), D ** -0.5, 0.1875, ((2, 8),))
    dw_weight = scatter_about(streams_of[12], (KW, D), KW ** -0.5, 2.0, ((1, 8),))
    bn_scale = jnp.clip(1.0 + 0.18 * jax.random.normal(streams_of[13], (D,), jnp.float32), 0.1, 1.9)
    bn_shift = scatter_about(streams_of[14], (D,), 0.5, 2.5, ((0, 8),), jnp.float32)
    w_pw2 = scatter_about(streams_of[15], (D, D), D ** -0.5, 0.1875, ((0, 8),))
    return {"frame_rows": frame_rows, "route_owner": route_owner, "route_slot": route_slot, "frames": frames, "kv_cache": kv_cache, "conv_cache": conv_cache, "mig_owner": mig_owner, "ln1_gain": ln1_gain, "w_qkv": w_qkv, "w_out": w_out, "ln2_gain": ln2_gain, "w_pw1": w_pw1, "dw_weight": dw_weight, "bn_scale": bn_scale, "bn_shift": bn_shift, "w_pw2": w_pw2}


norm_eps = 1e-05

def normalize(values, gain_cols):
    model_width = values.shape[-1]
    row_mean = lax.optimization_barrier(jnp.sum(values, axis=-1)) / model_width
    spread = lax.optimization_barrier(jnp.sum(values * values, axis=-1)) / model_width - row_mean * row_mean
    return ((values - row_mean[:, None]) * lax.rsqrt(spread + norm_eps)[:, None] * gain_cols).astype(jnp.bfloat16)

def advance(history, fresh_rows, counts, frame_axis):
    joined = jnp.concatenate([history, fresh_rows], axis=frame_axis)
    keep_rows = history.shape[frame_axis]

    def take_one(single, start):
        return lax.dynamic_slice_in_dim(single, start, keep_rows, frame_axis - 1)
    return jax.vmap(take_one)(joined, counts.astype(jnp.int32))

def depthwise(history, glu_out, taps, bn_scale, bn_shift):
    joined = jnp.concatenate([history, glu_out], axis=1).astype(jnp.float32)
    frame_total = glu_out.shape[1]
    running = jnp.zeros(glu_out.shape, jnp.float32)
    for tap_index in range(taps.shape[0]):
        running = running + joined[:, tap_index:tap_index + frame_total, :] * taps[tap_index].astype(jnp.float32)
    return jax.nn.silu(running * bn_scale + bn_shift).astype(jnp.bfloat16)

def grouped_sum(left, right, groups):
    group_width = left.shape[1] // groups
    running = jnp.zeros((left.shape[0], right.shape[1]), jnp.float32)
    for group_index in range(groups):
        group_term = jnp.dot(left[:, group_index * group_width:(group_index + 1) * group_width], right[group_index * group_width:(group_index + 1) * group_width], preferred_element_type=jnp.float32)
        rounded = lax.optimization_barrier(group_term.astype(jnp.bfloat16))
        running = running + rounded.astype(jnp.float32)
    return running

def reference(frame_rows, route_owner, route_slot, frames, kv_cache, conv_cache, mig_owner, ln1_gain, w_qkv, w_out, ln2_gain, w_pw1, dw_weight, bn_scale, bn_shift, w_pw2):
    arranged = jnp.zeros_like(frame_rows).at[route_owner * S_OWN + route_slot].set(frame_rows)
    settled = S_OWN - MIG
    sender = jnp.arange(N_OWNER * MIG, dtype=jnp.int32) // MIG
    mover = jnp.arange(N_OWNER * MIG, dtype=jnp.int32) % MIG
    source_owner = jnp.zeros((N_OWNER * MIG,), jnp.int32).at[mig_owner * MIG + mover].set(sender)
    row_count = S_OWN * CH

    def owner_layer(owner_index):
        slot_index = jnp.arange(S_OWN, dtype=jnp.int32)
        mover_slot = jnp.maximum(slot_index - settled, 0)
        anchor = jnp.where(slot_index < settled, owner_index, source_owner[owner_index * MIG + mover_slot])
        source_row = anchor * S_OWN + slot_index
        kv_state = kv_cache[source_row]
        conv_state = conv_cache[source_row]
        inputs = lax.dynamic_slice_in_dim(arranged, owner_index * S_OWN, S_OWN, 0)
        frame_counts = lax.dynamic_slice_in_dim(frames, owner_index * S_OWN, S_OWN, 0)
        outputs = []
        for block_index in range(BLOCKS):
            counts = jnp.clip(frame_counts - block_index * CH, 0, CH).astype(jnp.int32)
            plain_rows = inputs[:, block_index * CH:(block_index + 1) * CH].reshape(row_count, D).astype(jnp.float32)
            normed = normalize(plain_rows, ln1_gain)
            projected = jnp.dot(normed, w_qkv.reshape(D, H * 3 * HD), preferred_element_type=jnp.float32)
            projected = projected.reshape(S_OWN, CH, H, 3 * HD)
            queries = projected[..., :HD].astype(jnp.bfloat16)
            fresh_kv = jnp.transpose(projected[..., HD:].astype(jnp.bfloat16), (0, 2, 1, 3))
            memory = jnp.concatenate([kv_state, fresh_kv], axis=2).astype(jnp.float32)
            scores = jnp.einsum('sqhd,shkd->shqk', queries.astype(jnp.float32), memory[..., :HD]) * HD ** (-0.5)
            position = jnp.arange(L + CH, dtype=jnp.int32)
            live_keys = position[None, :] < L + counts[:, None]
            scores = jnp.where(live_keys[:, None, None, :], scores, -1e+30)
            row_max = lax.optimization_barrier(jnp.max(scores, axis=-1, keepdims=True))
            weights = jnp.exp(scores - row_max)
            probabilities = (weights / lax.optimization_barrier(jnp.sum(weights, axis=-1, keepdims=True))).astype(jnp.bfloat16)
            context = jnp.einsum('shqk,shkd->sqhd', probabilities.astype(jnp.float32), memory[..., HD:])
            context = context.astype(jnp.bfloat16).reshape(row_count, H * HD)
            residual = plain_rows + grouped_sum(context, w_out, N_INGEST)
            normed2 = normalize(residual, ln2_gain)
            mixed = jnp.dot(normed2, w_pw1.reshape(D, 2 * D), preferred_element_type=jnp.float32)
            glu_out = (mixed[:, :D] * jax.nn.sigmoid(mixed[:, D:])).astype(jnp.bfloat16).reshape(S_OWN, CH, D)
            activated = depthwise(conv_state, glu_out, dw_weight, bn_scale, bn_shift).reshape(row_count, D)
            result = residual + grouped_sum(activated, w_pw2, N_INGEST)
            live_rows = jnp.arange(CH, dtype=jnp.int32)[None, :] < counts[:, None]
            result = jnp.where(live_rows[:, :, None], result.reshape(S_OWN, CH, D), 0.0)
            outputs.append(result.astype(jnp.bfloat16))
            kv_state = advance(kv_state, fresh_kv, counts, 2)
            conv_state = advance(conv_state, glu_out, counts, 1)
        return (jnp.concatenate(outputs, axis=1), kv_state, conv_state)
    layer_out, kv_next, conv_next = lax.map(owner_layer, jnp.arange(N_OWNER, dtype=jnp.int32))
    return (layer_out.reshape(UTTS, BLOCKS * CH, D), kv_next.reshape(UTTS, H, L, 2 * HD), conv_next.reshape(UTTS, KT, D))
```

```python
import jax
import jax.numpy as jnp
from jax import lax
from jax.sharding import PartitionSpec as P

BLOCKS = 2


norm_eps = 1e-05


def normalize(values, gain_cols):
    model_width = values.shape[-1]
    row_mean = jnp.sum(values, axis=-1, keepdims=True) / model_width
    spread = jnp.sum(values * values, axis=-1, keepdims=True) / model_width - row_mean * row_mean
    return ((values - row_mean) * lax.rsqrt(spread + norm_eps) * gain_cols).astype(jnp.bfloat16)


def one_hot_rows(table, rows):
    return jnp.dot(
        table.astype(jnp.bfloat16), rows, preferred_element_type=jnp.float32
    ).astype(jnp.bfloat16)


def grouped_terms(left_groups, right_groups):
    terms = jnp.einsum(
        "grc,gcn->grn", left_groups, right_groups, preferred_element_type=jnp.float32
    ).astype(jnp.bfloat16)
    return jnp.sum(terms.astype(jnp.float32), axis=0)


def shards(
    frame_rows,
    route_owner,
    route_slot,
    frames,
    kv_cache,
    conv_cache,
    mig_owner,
    ln1_gain,
    w_qkv,
    w_out,
    ln2_gain,
    w_pw1,
    dw_weight,
    bn_scale,
    bn_shift,
    w_pw2,
):
    owners = lax.axis_size("owner")
    groups = lax.axis_size("ingest")
    me = lax.axis_index("ingest")
    utterances, frame_span, local_width = frame_rows.shape
    model_width = w_qkv.shape[0]
    head_dim = w_qkv.shape[2] // 3
    cache_len = kv_cache.shape[2]
    conv_len = conv_cache.shape[1]
    taps = dw_weight.shape[0]
    horizon = frame_span // BLOCKS
    moving = mig_owner.shape[0]
    settled = utterances - moving
    lanes = 128

    w_out_full = lax.all_gather(w_out, "ingest", axis=0, tiled=True)
    w_pw2_cols = lax.all_to_all(
        w_pw2.reshape(local_width, groups, local_width).transpose(1, 0, 2),
        "ingest",
        split_axis=0,
        concat_axis=0,
        tiled=True,
    )

    dest = jnp.arange(owners, dtype=jnp.int32)
    frame_flat = frame_rows.reshape(utterances, frame_span * local_width)
    slot_tag = jnp.broadcast_to(
        (route_slot + 1).astype(jnp.bfloat16)[:, None], (utterances, lanes)
    )
    frame_send = one_hot_rows(
        dest[:, None] == route_owner[None, :], jnp.concatenate([frame_flat, slot_tag], axis=1)
    )
    kv_width = cache_len * 2 * head_dim
    conv_width = conv_len * local_width
    mover_tag = jnp.broadcast_to(
        (jnp.arange(moving, dtype=jnp.int32) + 1).astype(jnp.bfloat16)[:, None], (moving, lanes)
    )
    cache_rows = jnp.concatenate(
        [
            kv_cache[settled:].reshape(moving, kv_width),
            conv_cache[settled:].reshape(moving, conv_width),
            mover_tag,
        ],
        axis=1,
    )
    cache_send = one_hot_rows(dest[:, None] == mig_owner[None, :], cache_rows)
    frame_cols = frame_send.shape[1]
    arrived = lax.all_to_all(
        jnp.concatenate([frame_send, cache_send], axis=1),
        "owner",
        split_axis=0,
        concat_axis=0,
        tiled=True,
    )
    frame_part = frame_span * local_width
    got_slot = arrived[:, frame_part].astype(jnp.int32)
    slots = jnp.arange(utterances, dtype=jnp.int32)
    arranged = one_hot_rows(
        slots[:, None] + 1 == got_slot[None, :], arrived[:, :frame_part]
    ).reshape(utterances, frame_span, local_width)
    got_mover = arrived[:, frame_cols + kv_width + conv_width].astype(jnp.int32)
    movers = jnp.arange(moving, dtype=jnp.int32)
    moved = one_hot_rows(
        movers[:, None] + 1 == got_mover[None, :],
        arrived[:, frame_cols : frame_cols + kv_width + conv_width],
    )
    kv_state = jnp.concatenate(
        [
            kv_cache[:settled].reshape(settled, cache_len, 2 * head_dim),
            moved[:, :kv_width].reshape(moving, cache_len, 2 * head_dim),
        ],
        axis=0,
    )
    conv_state = jnp.concatenate(
        [conv_cache[:settled], moved[:, kv_width:].reshape(moving, conv_len, local_width)],
        axis=0,
    )

    x_all = lax.all_gather(arranged, "ingest", axis=0, tiled=False)
    x_rows = x_all.transpose(1, 2, 0, 3).reshape(utterances, frame_span, model_width)
    x_rows = x_rows.astype(jnp.float32)
    normed = normalize(x_rows, ln1_gain)
    projected = jnp.dot(
        normed, w_qkv.reshape(model_width, 3 * head_dim), preferred_element_type=jnp.float32
    )
    queries = projected[..., :head_dim].astype(jnp.bfloat16)
    fresh = projected[..., head_dim:].astype(jnp.bfloat16)

    memory = jnp.concatenate([kv_state, fresh], axis=1)
    keys_total = memory.shape[1]
    scores = jnp.einsum(
        "sqd,skd->sqk", queries, memory[..., :head_dim], preferred_element_type=jnp.float32
    ) * head_dim ** (-0.5)
    frame_index = jnp.arange(frame_span, dtype=jnp.int32)
    block_of = frame_index // horizon
    low = block_of * horizon
    high = cache_len + jnp.minimum(frames[:, None], (block_of[None, :] + 1) * horizon)
    position = jnp.arange(keys_total, dtype=jnp.int32)
    live_keys = (position[None, None, :] >= low[None, :, None]) & (
        position[None, None, :] < high[:, :, None]
    )
    scores = jnp.where(live_keys, scores, -1e30)
    row_max = jnp.max(scores, axis=-1, keepdims=True)
    weights = jnp.exp(scores - row_max)
    probabilities = (weights / jnp.sum(weights, axis=-1, keepdims=True)).astype(jnp.bfloat16)
    context = jnp.einsum(
        "sqk,skd->sqd", probabilities, memory[..., head_dim:], preferred_element_type=jnp.float32
    ).astype(jnp.bfloat16)

    ctx_all = lax.all_gather(context, "ingest", axis=0, tiled=False)
    row_count = utterances * frame_span
    attn = grouped_terms(
        ctx_all.reshape(groups, row_count, head_dim),
        w_out_full.reshape(groups, head_dim, model_width),
    )
    residual = x_rows.reshape(row_count, model_width) + attn
    normed2 = normalize(residual, ln2_gain)
    mixed = jnp.dot(
        normed2, w_pw1.reshape(model_width, 2 * local_width), preferred_element_type=jnp.float32
    )
    glu_out = (mixed[:, :local_width] * jax.nn.sigmoid(mixed[:, local_width:])).astype(
        jnp.bfloat16
    )
    glu_out = glu_out.reshape(utterances, frame_span, local_width)

    joined = jnp.concatenate([conv_state, glu_out], axis=1)
    joined_f = joined.astype(jnp.float32)
    running = jnp.zeros((utterances, frame_span, local_width), jnp.float32)
    for tap_index in range(taps):
        running = running + joined_f[:, tap_index : tap_index + frame_span, :] * dw_weight[
            tap_index
        ].astype(jnp.float32)
    activated = jax.nn.silu(running * bn_scale + bn_shift).astype(jnp.bfloat16)

    act_all = lax.all_gather(activated, "ingest", axis=0, tiled=False)
    conv_terms = grouped_terms(act_all.reshape(groups, row_count, local_width), w_pw2_cols)
    residual_own = lax.dynamic_slice_in_dim(residual, me * local_width, local_width, 1)
    result = (residual_own + conv_terms).reshape(utterances, frame_span, local_width)
    live_rows = frame_index[None, :] < frames[:, None]
    layer_out = jnp.where(live_rows[:, :, None], result, 0.0).astype(jnp.bfloat16)

    keep = jnp.arange(cache_len, dtype=jnp.int32)
    kv_pick = position[None, None, :] == keep[None, :, None] + frames[:, None, None]
    kv_next = jnp.einsum(
        "srp,spd->srd", kv_pick.astype(jnp.bfloat16), memory, preferred_element_type=jnp.float32
    ).astype(jnp.bfloat16)
    conv_keep = jnp.arange(conv_len, dtype=jnp.int32)
    conv_pos = jnp.arange(joined.shape[1], dtype=jnp.int32)
    conv_pick = conv_pos[None, None, :] == conv_keep[None, :, None] + frames[:, None, None]
    conv_next = jnp.einsum(
        "srp,spd->srd", conv_pick.astype(jnp.bfloat16), joined, preferred_element_type=jnp.float32
    ).astype(jnp.bfloat16)
    return (layer_out, kv_next.reshape(kv_cache.shape), conv_next)


def solution(mesh):
    in_specs = (
        P("owner", None, "ingest"),
        P("owner"),
        P("owner"),
        P("owner"),
        P("owner", "ingest", None, None),
        P("owner", None, "ingest"),
        P("owner"),
        P(),
        P(None, "ingest", None),
        P("ingest", None),
        P(),
        P(None, None, "ingest"),
        P(None, "ingest"),
        P("ingest"),
        P("ingest"),
        P("ingest", None),
    )
    out_specs = (
        P("owner", None, "ingest"),
        P("owner", "ingest", None, None),
        P("owner", None, "ingest"),
    )
    return jax.shard_map(shards, mesh=mesh, in_specs=in_specs, out_specs=out_specs, check_vma=False)
```

```python
import jax
import jax.numpy as jnp
from jax import lax
from jax.sharding import PartitionSpec as P

BLOCKS = 2


norm_eps = 1e-05


def normalize(values, gain_cols):
    model_width = values.shape[-1]
    row_mean = jnp.sum(values, axis=-1, keepdims=True) / model_width
    spread = jnp.sum(values * values, axis=-1, keepdims=True) / model_width - row_mean * row_mean
    return ((values - row_mean) * lax.rsqrt(spread + norm_eps) * gain_cols).astype(jnp.bfloat16)


def shards(
    frame_rows,
    route_owner,
    route_slot,
    frames,
    kv_cache,
    conv_cache,
    mig_owner,
    ln1_gain,
    w_qkv,
    w_out,
    ln2_gain,
    w_pw1,
    dw_weight,
    bn_scale,
    bn_shift,
    w_pw2,
):
    owners = lax.axis_size("owner")
    groups = lax.axis_size("ingest")
    me = lax.axis_index("ingest")
    utterances, frame_span, local_width = frame_rows.shape
    model_width = w_qkv.shape[0]
    head_dim = w_qkv.shape[2] // 3
    cache_len = kv_cache.shape[2]
    conv_len = conv_cache.shape[1]
    taps = dw_weight.shape[0]
    horizon = frame_span // BLOCKS
    moving = mig_owner.shape[0]
    settled = utterances - moving

    dest = jnp.arange(owners, dtype=jnp.int32)
    frame_pad = -(-(frame_span + 1) // 16) * 16
    slot_tag = jnp.broadcast_to(
        (route_slot + 1).astype(jnp.bfloat16)[:, None, None], (utterances, 1, local_width)
    )
    frame_rows_tagged = jnp.concatenate(
        [
            frame_rows,
            slot_tag,
            jnp.zeros((utterances, frame_pad - frame_span - 1, local_width), jnp.bfloat16),
        ],
        axis=1,
    )
    frame_send = jnp.einsum(
        "ds,stc->dtc",
        (dest[:, None] == route_owner[None, :]).astype(jnp.bfloat16),
        frame_rows_tagged,
        preferred_element_type=jnp.float32,
    ).astype(jnp.bfloat16)
    frame_got = lax.all_to_all(frame_send, "owner", split_axis=0, concat_axis=0, tiled=True)

    kv_lanes = 2 * head_dim
    conv_fold = conv_len * local_width // kv_lanes
    cache_used = cache_len + conv_fold + 1
    cache_pad = -(-cache_used // 16) * 16
    mover_tag = jnp.broadcast_to(
        (jnp.arange(moving, dtype=jnp.int32) + 1).astype(jnp.bfloat16)[:, None, None],
        (moving, 1, kv_lanes),
    )
    cache_rows = jnp.concatenate(
        [
            kv_cache[settled:, 0],
            conv_cache[settled:].reshape(moving, conv_fold, kv_lanes),
            mover_tag,
            jnp.zeros((moving, cache_pad - cache_used, kv_lanes), jnp.bfloat16),
        ],
        axis=1,
    )
    cache_send = jnp.einsum(
        "dj,jrc->drc",
        (dest[:, None] == mig_owner[None, :]).astype(jnp.bfloat16),
        cache_rows,
        preferred_element_type=jnp.float32,
    ).astype(jnp.bfloat16)
    cache_got = lax.all_to_all(cache_send, "owner", split_axis=0, concat_axis=0, tiled=True)

    got_slot = frame_got[:, frame_span, 0].astype(jnp.int32)
    slots = jnp.arange(utterances, dtype=jnp.int32)
    arranged = jnp.einsum(
        "so,otc->stc",
        (slots[:, None] + 1 == got_slot[None, :]).astype(jnp.bfloat16),
        frame_got[:, :frame_span],
        preferred_element_type=jnp.float32,
    ).astype(jnp.bfloat16)

    x_all = lax.all_gather(arranged, "ingest", axis=0, tiled=False)
    w_out_in, w_pw2_in, x_all = lax.optimization_barrier((w_out, w_pw2, x_all))
    w_out_full = lax.all_gather(w_out_in, "ingest", axis=0, tiled=True)
    w_pw2_full = lax.all_gather(w_pw2_in, "ingest", axis=0, tiled=True)
    x_rows = x_all.transpose(1, 2, 0, 3).reshape(utterances, frame_span, model_width)
    x_rows = x_rows.astype(jnp.float32)
    normed = normalize(x_rows, ln1_gain)
    projected = jnp.dot(
        normed, w_qkv.reshape(model_width, 3 * head_dim), preferred_element_type=jnp.float32
    )
    queries = projected[..., :head_dim].astype(jnp.bfloat16)
    fresh = projected[..., head_dim:].astype(jnp.bfloat16)
    w_out_full, w_pw2_full, queries, fresh = lax.optimization_barrier(
        (w_out_full, w_pw2_full, queries, fresh)
    )
    w_pw2_cols = lax.dynamic_slice_in_dim(w_pw2_full, me * local_width, local_width, 1).reshape(
        groups, local_width, local_width
    )

    got_mover = cache_got[:, cache_used - 1, 0].astype(jnp.int32)
    movers = jnp.arange(moving, dtype=jnp.int32)
    moved = jnp.einsum(
        "jo,orc->jrc",
        (movers[:, None] + 1 == got_mover[None, :]).astype(jnp.bfloat16),
        cache_got[:, : cache_used - 1],
        preferred_element_type=jnp.float32,
    ).astype(jnp.bfloat16)
    kv_state = jnp.concatenate([kv_cache[:settled, 0], moved[:, :cache_len]], axis=0)
    conv_state = jnp.concatenate(
        [conv_cache[:settled], moved[:, cache_len:].reshape(moving, conv_len, local_width)],
        axis=0,
    )

    memory = jnp.concatenate([kv_state, fresh], axis=1)
    keys_total = memory.shape[1]
    scores = jnp.einsum(
        "sqd,skd->sqk", queries, memory[..., :head_dim], preferred_element_type=jnp.float32
    ) * head_dim ** (-0.5)
    frame_index = jnp.arange(frame_span, dtype=jnp.int32)
    block_of = frame_index // horizon
    low = block_of * horizon
    high = cache_len + jnp.minimum(frames[:, None], (block_of[None, :] + 1) * horizon)
    position = jnp.arange(keys_total, dtype=jnp.int32)
    live_keys = (position[None, None, :] >= low[None, :, None]) & (
        position[None, None, :] < high[:, :, None]
    )
    scores = jnp.where(live_keys, scores, -1e30)
    row_max = jnp.max(scores, axis=-1, keepdims=True)
    weights = jnp.exp(scores - row_max)
    probabilities = (weights / jnp.sum(weights, axis=-1, keepdims=True)).astype(jnp.bfloat16)
    context = jnp.einsum(
        "sqk,skd->sqd", probabilities, memory[..., head_dim:], preferred_element_type=jnp.float32
    ).astype(jnp.bfloat16)

    ctx_all = lax.all_gather(context, "ingest", axis=0, tiled=False)
    row_count = utterances * frame_span
    attn = jnp.einsum(
        "grc,gcn->rn",
        ctx_all.reshape(groups, row_count, head_dim),
        w_out_full.reshape(groups, head_dim, model_width),
        preferred_element_type=jnp.float32,
    )
    residual = x_rows.reshape(row_count, model_width) + attn
    normed2 = normalize(residual, ln2_gain)
    mixed = jnp.dot(
        normed2, w_pw1.reshape(model_width, 2 * local_width), preferred_element_type=jnp.float32
    )
    glu_out = (mixed[:, :local_width] * jax.nn.sigmoid(mixed[:, local_width:])).astype(
        jnp.bfloat16
    )
    glu_out = glu_out.reshape(utterances, frame_span, local_width)

    joined = jnp.concatenate([conv_state, glu_out], axis=1)
    joined_f = joined.astype(jnp.float32)
    running = jnp.zeros((utterances, frame_span, local_width), jnp.float32)
    for tap_index in range(taps):
        running = running + joined_f[:, tap_index : tap_index + frame_span, :] * dw_weight[
            tap_index
        ].astype(jnp.float32)
    activated = jax.nn.silu(running * bn_scale + bn_shift).astype(jnp.bfloat16)

    act_all = lax.all_gather(activated, "ingest", axis=0, tiled=False)
    conv_terms = jnp.einsum(
        "grc,gcn->rn",
        act_all.reshape(groups, row_count, local_width),
        w_pw2_cols,
        preferred_element_type=jnp.float32,
    )
    residual_own = lax.dynamic_slice_in_dim(residual, me * local_width, local_width, 1)
    result = (residual_own + conv_terms).reshape(utterances, frame_span, local_width)
    live_rows = frame_index[None, :] < frames[:, None]
    layer_out = jnp.where(live_rows[:, :, None], result, 0.0).astype(jnp.bfloat16)

    keep = jnp.arange(cache_len, dtype=jnp.int32)
    kv_pick = position[None, None, :] == keep[None, :, None] + frames[:, None, None]
    kv_next = jnp.einsum(
        "srp,spd->srd", kv_pick.astype(jnp.bfloat16), memory, preferred_element_type=jnp.float32
    ).astype(jnp.bfloat16)
    conv_keep = jnp.arange(conv_len, dtype=jnp.int32)
    conv_pos = jnp.arange(joined.shape[1], dtype=jnp.int32)
    conv_pick = conv_pos[None, None, :] == conv_keep[None, :, None] + frames[:, None, None]
    conv_next = jnp.einsum(
        "srp,spd->srd", conv_pick.astype(jnp.bfloat16), joined, preferred_element_type=jnp.float32
    ).astype(jnp.bfloat16)
    return (layer_out, kv_next.reshape(kv_cache.shape), conv_next)


def solution(mesh):
    in_specs = (
        P("owner", None, "ingest"),
        P("owner"),
        P("owner"),
        P("owner"),
        P("owner", "ingest", None, None),
        P("owner", None, "ingest"),
        P("owner"),
        P(),
        P(None, "ingest", None),
        P("ingest", None),
        P(),
        P(None, None, "ingest"),
        P(None, "ingest"),
        P("ingest"),
        P("ingest"),
        P("ingest", None),
    )
    out_specs = (
        P("owner", None, "ingest"),
        P("owner", "ingest", None, None),
        P("owner", None, "ingest"),
    )
    return jax.shard_map(shards, mesh=mesh, in_specs=in_specs, out_specs=out_specs, check_vma=False)
```

```python
import jax
import jax.numpy as jnp
from jax import lax
from jax.sharding import PartitionSpec as P

BLOCKS = 2


norm_eps = 1e-05


def normalize(values, gain_cols):
    model_width = values.shape[-1]
    row_mean = jnp.sum(values, axis=-1, keepdims=True) / model_width
    spread = jnp.sum(values * values, axis=-1, keepdims=True) / model_width - row_mean * row_mean
    return ((values - row_mean) * lax.rsqrt(spread + norm_eps) * gain_cols).astype(jnp.bfloat16)


def shards(
    frame_rows,
    route_owner,
    route_slot,
    frames,
    kv_cache,
    conv_cache,
    mig_owner,
    ln1_gain,
    w_qkv,
    w_out,
    ln2_gain,
    w_pw1,
    dw_weight,
    bn_scale,
    bn_shift,
    w_pw2,
):
    owners = lax.axis_size("owner")
    groups = lax.axis_size("ingest")
    me = lax.axis_index("ingest")
    utterances, frame_span, local_width = frame_rows.shape
    model_width = w_qkv.shape[0]
    head_dim = w_qkv.shape[2] // 3
    cache_len = kv_cache.shape[2]
    conv_len = conv_cache.shape[1]
    taps = dw_weight.shape[0]
    horizon = frame_span // BLOCKS
    moving = mig_owner.shape[0]
    settled = utterances - moving

    dest = jnp.arange(owners, dtype=jnp.int32)
    frame_pad = -(-(frame_span + 1) // 16) * 16
    slot_tag = jnp.broadcast_to(
        (route_slot + 1).astype(jnp.bfloat16)[:, None, None], (utterances, 1, local_width)
    )
    frame_rows_tagged = jnp.concatenate(
        [
            frame_rows,
            slot_tag,
            jnp.zeros((utterances, frame_pad - frame_span - 1, local_width), jnp.bfloat16),
        ],
        axis=1,
    )
    frame_send = jnp.einsum(
        "ds,stc->dtc",
        (dest[:, None] == route_owner[None, :]).astype(jnp.bfloat16),
        frame_rows_tagged,
        preferred_element_type=jnp.float32,
    ).astype(jnp.bfloat16)
    frame_got = lax.all_to_all(frame_send, "owner", split_axis=0, concat_axis=0, tiled=True)

    kv_lanes = 2 * head_dim
    conv_fold = conv_len * local_width // kv_lanes
    cache_used = cache_len + conv_fold + 1
    cache_pad = -(-cache_used // 16) * 16
    mover_tag = jnp.broadcast_to(
        (jnp.arange(moving, dtype=jnp.int32) + 1).astype(jnp.bfloat16)[:, None, None],
        (moving, 1, kv_lanes),
    )
    cache_rows = jnp.concatenate(
        [
            kv_cache[settled:, 0],
            conv_cache[settled:].reshape(moving, conv_fold, kv_lanes),
            mover_tag,
            jnp.zeros((moving, cache_pad - cache_used, kv_lanes), jnp.bfloat16),
        ],
        axis=1,
    )
    cache_send = jnp.einsum(
        "dj,jrc->drc",
        (dest[:, None] == mig_owner[None, :]).astype(jnp.bfloat16),
        cache_rows,
        preferred_element_type=jnp.float32,
    ).astype(jnp.bfloat16)
    cache_got = lax.all_to_all(cache_send, "owner", split_axis=0, concat_axis=0, tiled=True)

    got_slot = frame_got[:, frame_span, 0].astype(jnp.int32)
    slots = jnp.arange(utterances, dtype=jnp.int32)
    arranged = jnp.einsum(
        "so,otc->stc",
        (slots[:, None] + 1 == got_slot[None, :]).astype(jnp.bfloat16),
        frame_got[:, :frame_span],
        preferred_element_type=jnp.float32,
    ).astype(jnp.bfloat16)

    x_all = lax.all_gather(arranged, "ingest", axis=0, tiled=False)
    w_out_full = lax.all_gather(w_out, "ingest", axis=0, tiled=True)
    w_pw1_all = lax.all_gather(w_pw1, "ingest", axis=0, tiled=False)
    dw_all = lax.all_gather(dw_weight, "ingest", axis=0, tiled=False)
    bn_all = lax.all_gather(jnp.stack([bn_scale, bn_shift]), "ingest", axis=0, tiled=False)
    x_rows = x_all.transpose(1, 2, 0, 3).reshape(utterances, frame_span, model_width)
    x_rows = x_rows.astype(jnp.float32)
    normed = normalize(x_rows, ln1_gain)
    projected = jnp.dot(
        normed, w_qkv.reshape(model_width, 3 * head_dim), preferred_element_type=jnp.float32
    )
    queries = projected[..., :head_dim].astype(jnp.bfloat16)
    fresh = projected[..., head_dim:].astype(jnp.bfloat16)
    w_out_full, w_pw1_all, dw_all, bn_all, queries, fresh = lax.optimization_barrier(
        (w_out_full, w_pw1_all, dw_all, bn_all, queries, fresh)
    )
    dw_full = dw_all.transpose(1, 0, 2).reshape(taps, model_width).astype(jnp.float32)
    bn_scale_full = bn_all[:, 0].reshape(model_width)
    bn_shift_full = bn_all[:, 1].reshape(model_width)

    got_mover = cache_got[:, cache_used - 1, 0].astype(jnp.int32)
    movers = jnp.arange(moving, dtype=jnp.int32)
    moved = jnp.einsum(
        "jo,orc->jrc",
        (movers[:, None] + 1 == got_mover[None, :]).astype(jnp.bfloat16),
        cache_got[:, : cache_used - 1],
        preferred_element_type=jnp.float32,
    ).astype(jnp.bfloat16)
    kv_state = jnp.concatenate([kv_cache[:settled, 0], moved[:, :cache_len]], axis=0)
    conv_state = jnp.concatenate(
        [conv_cache[:settled], moved[:, cache_len:].reshape(moving, conv_len, local_width)],
        axis=0,
    )

    memory = jnp.concatenate([kv_state, fresh], axis=1)
    keys_total = memory.shape[1]
    scores = jnp.einsum(
        "sqd,skd->sqk", queries, memory[..., :head_dim], preferred_element_type=jnp.float32
    ) * head_dim ** (-0.5)
    frame_index = jnp.arange(frame_span, dtype=jnp.int32)
    block_of = frame_index // horizon
    low = block_of * horizon
    high = cache_len + jnp.minimum(frames[:, None], (block_of[None, :] + 1) * horizon)
    position = jnp.arange(keys_total, dtype=jnp.int32)
    live_keys = (position[None, None, :] >= low[None, :, None]) & (
        position[None, None, :] < high[:, :, None]
    )
    scores = jnp.where(live_keys, scores, -1e30)
    row_max = jnp.max(scores, axis=-1, keepdims=True)
    weights = jnp.exp(scores - row_max)
    probabilities = (weights / jnp.sum(weights, axis=-1, keepdims=True)).astype(jnp.bfloat16)
    context = jnp.einsum(
        "sqk,skd->sqd", probabilities, memory[..., head_dim:], preferred_element_type=jnp.float32
    ).astype(jnp.bfloat16)

    ctx_all = lax.all_gather(context, "ingest", axis=0, tiled=False)
    row_count = utterances * frame_span
    attn = jnp.einsum(
        "grc,gcn->rn",
        ctx_all.reshape(groups, row_count, head_dim),
        w_out_full.reshape(groups, head_dim, model_width),
        preferred_element_type=jnp.float32,
    )
    residual = x_rows.reshape(row_count, model_width) + attn
    normed2 = normalize(residual, ln2_gain)
    w_pw2_cols = lax.all_to_all(
        w_pw2.reshape(local_width, groups, local_width).transpose(1, 0, 2),
        "ingest",
        split_axis=0,
        concat_axis=0,
        tiled=True,
    ).reshape(model_width, local_width)
    conv_all = lax.all_gather(conv_state, "ingest", axis=0, tiled=False)
    conv_full = conv_all.transpose(1, 2, 0, 3).reshape(utterances, conv_len, model_width)
    mixed = jnp.einsum("rk,gkvc->rvgc", normed2, w_pw1_all, preferred_element_type=jnp.float32)
    mixed = mixed.reshape(row_count, 2, model_width)
    glu_full = (mixed[:, 0] * jax.nn.sigmoid(mixed[:, 1])).astype(jnp.bfloat16)
    glu_full = glu_full.reshape(utterances, frame_span, model_width)

    joined_full = jnp.concatenate([conv_full, glu_full], axis=1).astype(jnp.float32)
    running = jnp.zeros((utterances, frame_span, model_width), jnp.float32)
    for tap_index in range(taps):
        running = running + joined_full[:, tap_index : tap_index + frame_span, :] * dw_full[
            tap_index
        ]
    activated = jax.nn.silu(running * bn_scale_full + bn_shift_full).astype(jnp.bfloat16)
    conv_terms = jnp.dot(
        activated.reshape(row_count, model_width), w_pw2_cols, preferred_element_type=jnp.float32
    )
    glu_out = lax.dynamic_slice_in_dim(glu_full, me * local_width, local_width, 2)
    joined = jnp.concatenate([conv_state, glu_out], axis=1)
    residual_own = lax.dynamic_slice_in_dim(residual, me * local_width, local_width, 1)
    result = (residual_own + conv_terms).reshape(utterances, frame_span, local_width)
    live_rows = frame_index[None, :] < frames[:, None]
    layer_out = jnp.where(live_rows[:, :, None], result, 0.0).astype(jnp.bfloat16)

    keep = jnp.arange(cache_len, dtype=jnp.int32)
    kv_pick = position[None, None, :] == keep[None, :, None] + frames[:, None, None]
    kv_next = jnp.einsum(
        "srp,spd->srd", kv_pick.astype(jnp.bfloat16), memory, preferred_element_type=jnp.float32
    ).astype(jnp.bfloat16)
    conv_keep = jnp.arange(conv_len, dtype=jnp.int32)
    conv_pos = jnp.arange(joined.shape[1], dtype=jnp.int32)
    conv_pick = conv_pos[None, None, :] == conv_keep[None, :, None] + frames[:, None, None]
    conv_next = jnp.einsum(
        "srp,spd->srd", conv_pick.astype(jnp.bfloat16), joined, preferred_element_type=jnp.float32
    ).astype(jnp.bfloat16)
    return (layer_out, kv_next.reshape(kv_cache.shape), conv_next)


def solution(mesh):
    in_specs = (
        P("owner", None, "ingest"),
        P("owner"),
        P("owner"),
        P("owner"),
        P("owner", "ingest", None, None),
        P("owner", None, "ingest"),
        P("owner"),
        P(),
        P(None, "ingest", None),
        P("ingest", None),
        P(),
        P(None, None, "ingest"),
        P(None, "ingest"),
        P("ingest"),
        P("ingest"),
        P("ingest", None),
    )
    out_specs = (
        P("owner", None, "ingest"),
        P("owner", "ingest", None, None),
        P("owner", None, "ingest"),
    )
    return jax.shard_map(shards, mesh=mesh, in_specs=in_specs, out_specs=out_specs, check_vma=False)
```

```python
import jax
import jax.numpy as jnp
from jax import lax
from jax.sharding import PartitionSpec as P

BLOCKS = 2


norm_eps = 1e-05


def normalize(values, gain_cols):
    model_width = values.shape[-1]
    row_mean = jnp.sum(values, axis=-1, keepdims=True) / model_width
    spread = jnp.sum(values * values, axis=-1, keepdims=True) / model_width - row_mean * row_mean
    return ((values - row_mean) * lax.rsqrt(spread + norm_eps) * gain_cols).astype(jnp.bfloat16)


def shards(
    frame_rows,
    route_owner,
    route_slot,
    frames,
    kv_cache,
    conv_cache,
    mig_owner,
    ln1_gain,
    w_qkv,
    w_out,
    ln2_gain,
    w_pw1,
    dw_weight,
    bn_scale,
    bn_shift,
    w_pw2,
):
    owners = lax.axis_size("owner")
    groups = lax.axis_size("ingest")
    me = lax.axis_index("ingest")
    utterances, frame_span, local_width = frame_rows.shape
    model_width = w_qkv.shape[0]
    head_dim = w_qkv.shape[2] // 3
    cache_len = kv_cache.shape[2]
    conv_len = conv_cache.shape[1]
    taps = dw_weight.shape[0]
    horizon = frame_span // BLOCKS
    moving = mig_owner.shape[0]
    settled = utterances - moving

    dest = jnp.arange(owners, dtype=jnp.int32)
    frame_pad = -(-(frame_span + 1) // 16) * 16
    slot_tag = jnp.broadcast_to(
        (route_slot + 1).astype(jnp.bfloat16)[:, None, None], (utterances, 1, local_width)
    )
    frame_rows_tagged = jnp.concatenate(
        [
            frame_rows,
            slot_tag,
            jnp.zeros((utterances, frame_pad - frame_span - 1, local_width), jnp.bfloat16),
        ],
        axis=1,
    )
    frame_send = jnp.einsum(
        "ds,stc->dtc",
        (dest[:, None] == route_owner[None, :]).astype(jnp.bfloat16),
        frame_rows_tagged,
        preferred_element_type=jnp.float32,
    ).astype(jnp.bfloat16)

    kv_lanes = 2 * head_dim
    conv_fold = conv_len * local_width // kv_lanes
    cache_used = cache_len + conv_fold + 1
    cache_pad = -(-cache_used // 16) * 16
    mover_tag = jnp.broadcast_to(
        (jnp.arange(moving, dtype=jnp.int32) + 1).astype(jnp.bfloat16)[:, None, None],
        (moving, 1, kv_lanes),
    )
    cache_rows = jnp.concatenate(
        [
            kv_cache[settled:, 0],
            conv_cache[settled:].reshape(moving, conv_fold, kv_lanes),
            mover_tag,
            jnp.zeros((moving, cache_pad - cache_used, kv_lanes), jnp.bfloat16),
        ],
        axis=1,
    )
    cache_send = jnp.einsum(
        "dj,jrc->drc",
        (dest[:, None] == mig_owner[None, :]).astype(jnp.bfloat16),
        cache_rows,
        preferred_element_type=jnp.float32,
    ).astype(jnp.bfloat16)
    frame_send, cache_send = lax.optimization_barrier((frame_send, cache_send))
    frame_got = lax.all_to_all(frame_send, "owner", split_axis=0, concat_axis=0, tiled=True)
    cache_got = lax.all_to_all(cache_send, "owner", split_axis=0, concat_axis=0, tiled=True)

    got_slot = frame_got[:, frame_span, 0].astype(jnp.int32)
    slots = jnp.arange(utterances, dtype=jnp.int32)
    frame_from = jnp.argmax(slots[:, None] + 1 == got_slot[None, :], axis=1)
    arranged = frame_got[frame_from, :frame_span]

    x_all = lax.all_gather(arranged, "ingest", axis=0, tiled=False)
    w_out_in, w_pw2_in, x_all = lax.optimization_barrier((w_out, w_pw2, x_all))
    w_out_full = lax.all_gather(w_out_in, "ingest", axis=0, tiled=True)
    w_pw2_full = lax.all_gather(w_pw2_in, "ingest", axis=0, tiled=True)
    x_rows = x_all.transpose(1, 2, 0, 3).reshape(utterances, frame_span, model_width)
    x_rows = x_rows.astype(jnp.float32)
    normed = normalize(x_rows, ln1_gain)
    projected = jnp.dot(
        normed, w_qkv.reshape(model_width, 3 * head_dim), preferred_element_type=jnp.float32
    )
    queries = projected[..., :head_dim].astype(jnp.bfloat16)
    fresh = projected[..., head_dim:].astype(jnp.bfloat16)
    w_out_full, w_pw2_full, queries, fresh = lax.optimization_barrier(
        (w_out_full, w_pw2_full, queries, fresh)
    )
    w_pw2_cols = lax.dynamic_slice_in_dim(w_pw2_full, me * local_width, local_width, 1).reshape(
        groups, local_width, local_width
    )

    got_mover = cache_got[:, cache_used - 1, 0].astype(jnp.int32)
    movers = jnp.arange(moving, dtype=jnp.int32)
    cache_from = jnp.argmax(movers[:, None] + 1 == got_mover[None, :], axis=1)
    moved = cache_got[cache_from, : cache_used - 1]
    kv_state = jnp.concatenate([kv_cache[:settled, 0], moved[:, :cache_len]], axis=0)
    conv_state = jnp.concatenate(
        [conv_cache[:settled], moved[:, cache_len:].reshape(moving, conv_len, local_width)],
        axis=0,
    )

    memory = jnp.concatenate([kv_state, fresh], axis=1)
    keys_total = memory.shape[1]
    scores = jnp.einsum(
        "sqd,skd->sqk", queries, memory[..., :head_dim], preferred_element_type=jnp.float32
    ) * head_dim ** (-0.5)
    frame_index = jnp.arange(frame_span, dtype=jnp.int32)
    block_of = frame_index // horizon
    low = block_of * horizon
    high = cache_len + jnp.minimum(frames[:, None], (block_of[None, :] + 1) * horizon)
    position = jnp.arange(keys_total, dtype=jnp.int32)
    live_keys = (position[None, None, :] >= low[None, :, None]) & (
        position[None, None, :] < high[:, :, None]
    )
    scores = jnp.where(live_keys, scores, -1e30)
    row_max = jnp.max(scores, axis=-1, keepdims=True)
    weights = jnp.exp(scores - row_max)
    probabilities = (weights / jnp.sum(weights, axis=-1, keepdims=True)).astype(jnp.bfloat16)
    context = jnp.einsum(
        "sqk,skd->sqd", probabilities, memory[..., head_dim:], preferred_element_type=jnp.float32
    ).astype(jnp.bfloat16)

    ctx_all = lax.all_gather(context, "ingest", axis=0, tiled=False)
    row_count = utterances * frame_span
    attn = jnp.einsum(
        "grc,gcn->rn",
        ctx_all.reshape(groups, row_count, head_dim),
        w_out_full.reshape(groups, head_dim, model_width),
        preferred_element_type=jnp.float32,
    )
    residual = x_rows.reshape(row_count, model_width) + attn
    normed2 = normalize(residual, ln2_gain)
    mixed = jnp.dot(
        normed2, w_pw1.reshape(model_width, 2 * local_width), preferred_element_type=jnp.float32
    )
    glu_out = (mixed[:, :local_width] * jax.nn.sigmoid(mixed[:, local_width:])).astype(
        jnp.bfloat16
    )
    glu_out = glu_out.reshape(utterances, frame_span, local_width)

    joined = jnp.concatenate([conv_state, glu_out], axis=1)
    joined_f = joined.astype(jnp.float32)
    running = jnp.zeros((utterances, frame_span, local_width), jnp.float32)
    for tap_index in range(taps):
        running = running + joined_f[:, tap_index : tap_index + frame_span, :] * dw_weight[
            tap_index
        ].astype(jnp.float32)
    activated = jax.nn.silu(running * bn_scale + bn_shift).astype(jnp.bfloat16)

    act_all = lax.all_gather(activated, "ingest", axis=0, tiled=False)
    conv_terms = jnp.einsum(
        "grc,gcn->rn",
        act_all.reshape(groups, row_count, local_width),
        w_pw2_cols,
        preferred_element_type=jnp.float32,
    )
    residual_own = lax.dynamic_slice_in_dim(residual, me * local_width, local_width, 1)
    result = (residual_own + conv_terms).reshape(utterances, frame_span, local_width)
    live_rows = frame_index[None, :] < frames[:, None]
    layer_out = jnp.where(live_rows[:, :, None], result, 0.0).astype(jnp.bfloat16)

    keep = jnp.arange(cache_len, dtype=jnp.int32)
    kv_pick = position[None, None, :] == keep[None, :, None] + frames[:, None, None]
    kv_next = jnp.einsum(
        "srp,spd->srd", kv_pick.astype(jnp.bfloat16), memory, preferred_element_type=jnp.float32
    ).astype(jnp.bfloat16)
    conv_keep = jnp.arange(conv_len, dtype=jnp.int32)
    conv_pos = jnp.arange(joined.shape[1], dtype=jnp.int32)
    conv_pick = conv_pos[None, None, :] == conv_keep[None, :, None] + frames[:, None, None]
    conv_next = jnp.einsum(
        "srp,spd->srd", conv_pick.astype(jnp.bfloat16), joined, preferred_element_type=jnp.float32
    ).astype(jnp.bfloat16)
    return (layer_out, kv_next.reshape(kv_cache.shape), conv_next)


def solution(mesh):
    in_specs = (
        P("owner", None, "ingest"),
        P("owner"),
        P("owner"),
        P("owner"),
        P("owner", "ingest", None, None),
        P("owner", None, "ingest"),
        P("owner"),
        P(),
        P(None, "ingest", None),
        P("ingest", None),
        P(),
        P(None, None, "ingest"),
        P(None, "ingest"),
        P("ingest"),
        P("ingest"),
        P("ingest", None),
    )
    out_specs = (
        P("owner", None, "ingest"),
        P("owner", "ingest", None, None),
        P("owner", None, "ingest"),
    )
    return jax.shard_map(shards, mesh=mesh, in_specs=in_specs, out_specs=out_specs, check_vma=False)
```

```python
import jax
import jax.numpy as jnp
from jax import lax
from jax.sharding import PartitionSpec as P

BLOCKS = 2
CHUNK_MIN = 19


norm_eps = 1e-05


def normalize(values, gain_cols):
    model_width = values.shape[-1]
    row_mean = jnp.sum(values, axis=-1, keepdims=True) / model_width
    spread = jnp.sum(values * values, axis=-1, keepdims=True) / model_width - row_mean * row_mean
    return ((values - row_mean) * lax.rsqrt(spread + norm_eps) * gain_cols).astype(jnp.bfloat16)


def shards(
    frame_rows,
    route_owner,
    route_slot,
    frames,
    kv_cache,
    conv_cache,
    mig_owner,
    ln1_gain,
    w_qkv,
    w_out,
    ln2_gain,
    w_pw1,
    dw_weight,
    bn_scale,
    bn_shift,
    w_pw2,
):
    owners = lax.axis_size("owner")
    groups = lax.axis_size("ingest")
    me = lax.axis_index("ingest")
    utterances, frame_span, local_width = frame_rows.shape
    model_width = w_qkv.shape[0]
    head_dim = w_qkv.shape[2] // 3
    cache_len = kv_cache.shape[2]
    conv_len = conv_cache.shape[1]
    taps = dw_weight.shape[0]
    horizon = frame_span // BLOCKS
    moving = mig_owner.shape[0]
    settled = utterances - moving

    dest = jnp.arange(owners, dtype=jnp.int32)
    frame_pad = -(-(frame_span + 1) // 16) * 16
    slot_tag = jnp.broadcast_to(
        (route_slot + 1).astype(jnp.bfloat16)[:, None, None], (utterances, 1, local_width)
    )
    frame_rows_tagged = jnp.concatenate(
        [
            frame_rows,
            slot_tag,
            jnp.zeros((utterances, frame_pad - frame_span - 1, local_width), jnp.bfloat16),
        ],
        axis=1,
    )
    frame_send = jnp.einsum(
        "ds,stc->dtc",
        (dest[:, None] == route_owner[None, :]).astype(jnp.bfloat16),
        frame_rows_tagged,
        preferred_element_type=jnp.float32,
    ).astype(jnp.bfloat16)
    frame_got = lax.all_to_all(frame_send, "owner", split_axis=0, concat_axis=0, tiled=True)

    kv_lanes = 2 * head_dim
    conv_fold = conv_len * local_width // kv_lanes
    cache_used = cache_len + conv_fold + 1
    cache_pad = -(-cache_used // 16) * 16
    mover_tag = jnp.broadcast_to(
        (jnp.arange(moving, dtype=jnp.int32) + 1).astype(jnp.bfloat16)[:, None, None],
        (moving, 1, kv_lanes),
    )
    cache_rows = jnp.concatenate(
        [
            kv_cache[settled:, 0],
            conv_cache[settled:].reshape(moving, conv_fold, kv_lanes),
            mover_tag,
            jnp.zeros((moving, cache_pad - cache_used, kv_lanes), jnp.bfloat16),
        ],
        axis=1,
    )
    cache_send = jnp.einsum(
        "dj,jrc->drc",
        (dest[:, None] == mig_owner[None, :]).astype(jnp.bfloat16),
        cache_rows,
        preferred_element_type=jnp.float32,
    ).astype(jnp.bfloat16)
    cache_got = lax.all_to_all(cache_send, "owner", split_axis=0, concat_axis=0, tiled=True)

    got_slot = frame_got[:, frame_span, 0].astype(jnp.int32)
    slots = jnp.arange(utterances, dtype=jnp.int32)
    arranged = jnp.einsum(
        "so,otc->stc",
        (slots[:, None] + 1 == got_slot[None, :]).astype(jnp.bfloat16),
        frame_got[:, :frame_span],
        preferred_element_type=jnp.float32,
    ).astype(jnp.bfloat16)

    x_all = lax.all_gather(arranged, "ingest", axis=0, tiled=False)
    w_out_in, w_pw2_in, x_all = lax.optimization_barrier((w_out, w_pw2, x_all))
    w_out_full = lax.all_gather(w_out_in, "ingest", axis=0, tiled=True)
    w_pw2_full = lax.all_gather(w_pw2_in, "ingest", axis=0, tiled=True)
    x_rows = x_all.transpose(1, 2, 0, 3).reshape(utterances, frame_span, model_width)
    x_rows = x_rows.astype(jnp.float32)
    normed = normalize(x_rows, ln1_gain)
    projected = jnp.dot(
        normed, w_qkv.reshape(model_width, 3 * head_dim), preferred_element_type=jnp.float32
    )
    queries = projected[..., :head_dim].astype(jnp.bfloat16)
    fresh = projected[..., head_dim:].astype(jnp.bfloat16)
    w_out_full, w_pw2_full, queries, fresh = lax.optimization_barrier(
        (w_out_full, w_pw2_full, queries, fresh)
    )
    w_pw2_cols = lax.dynamic_slice_in_dim(w_pw2_full, me * local_width, local_width, 1).reshape(
        groups, local_width, local_width
    )

    got_mover = cache_got[:, cache_used - 1, 0].astype(jnp.int32)
    movers = jnp.arange(moving, dtype=jnp.int32)
    moved = jnp.einsum(
        "jo,orc->jrc",
        (movers[:, None] + 1 == got_mover[None, :]).astype(jnp.bfloat16),
        cache_got[:, : cache_used - 1],
        preferred_element_type=jnp.float32,
    ).astype(jnp.bfloat16)
    kv_state = jnp.concatenate([kv_cache[:settled, 0], moved[:, :cache_len]], axis=0)
    conv_state = jnp.concatenate(
        [conv_cache[:settled], moved[:, cache_len:].reshape(moving, conv_len, local_width)],
        axis=0,
    )

    split = (utterances + 1) // 2
    chunk = max(split, CHUNK_MIN)
    pieces = []
    for lo, hi in ((0, split), (split, utterances)):
        extra = chunk - (hi - lo)
        grow = lambda a: jnp.pad(a[lo:hi], ((0, extra),) + ((0, 0),) * (a.ndim - 1))
        outs = chunk_layer(
            grow(queries), grow(fresh), grow(kv_state), grow(conv_state), grow(x_rows),
            grow(frames), w_out_full, w_pw1, w_pw2_cols, dw_weight, bn_scale, bn_shift,
            ln2_gain, me, groups, horizon,
        )
        pieces.append(tuple(o[: hi - lo] for o in outs))
    return tuple(jnp.concatenate(parts, axis=0) for parts in zip(*pieces))


def chunk_layer(
    queries, fresh, kv_state, conv_state, x_rows, frames, w_out_full, w_pw1, w_pw2_cols,
    dw_weight, bn_scale, bn_shift, ln2_gain, me, groups, horizon,
):
    utterances, frame_span, model_width = x_rows.shape
    head_dim = queries.shape[-1]
    cache_len = kv_state.shape[1]
    conv_len = conv_state.shape[1]
    local_width = conv_state.shape[2]
    taps = dw_weight.shape[0]
    memory = jnp.concatenate([kv_state, fresh], axis=1)
    keys_total = memory.shape[1]
    scores = jnp.einsum(
        "sqd,skd->sqk", queries, memory[..., :head_dim], preferred_element_type=jnp.float32
    ) * head_dim ** (-0.5)
    frame_index = jnp.arange(frame_span, dtype=jnp.int32)
    block_of = frame_index // horizon
    low = block_of * horizon
    high = cache_len + jnp.minimum(frames[:, None], (block_of[None, :] + 1) * horizon)
    position = jnp.arange(keys_total, dtype=jnp.int32)
    live_keys = (position[None, None, :] >= low[None, :, None]) & (
        position[None, None, :] < high[:, :, None]
    )
    scores = jnp.where(live_keys, scores, -1e30)
    row_max = jnp.max(scores, axis=-1, keepdims=True)
    weights = jnp.exp(scores - row_max)
    probabilities = (weights / jnp.sum(weights, axis=-1, keepdims=True)).astype(jnp.bfloat16)
    context = jnp.einsum(
        "sqk,skd->sqd", probabilities, memory[..., head_dim:], preferred_element_type=jnp.float32
    ).astype(jnp.bfloat16)

    ctx_all = lax.all_gather(context, "ingest", axis=0, tiled=False)
    row_count = utterances * frame_span
    attn = jnp.einsum(
        "grc,gcn->rn",
        ctx_all.reshape(groups, row_count, head_dim),
        w_out_full.reshape(groups, head_dim, model_width),
        preferred_element_type=jnp.float32,
    )
    residual = x_rows.reshape(row_count, model_width) + attn
    normed2 = normalize(residual, ln2_gain)
    mixed = jnp.dot(
        normed2, w_pw1.reshape(model_width, 2 * local_width), preferred_element_type=jnp.float32
    )
    glu_out = (mixed[:, :local_width] * jax.nn.sigmoid(mixed[:, local_width:])).astype(
        jnp.bfloat16
    )
    glu_out = glu_out.reshape(utterances, frame_span, local_width)

    joined = jnp.concatenate([conv_state, glu_out], axis=1)
    joined_f = joined.astype(jnp.float32)
    running = jnp.zeros((utterances, frame_span, local_width), jnp.float32)
    for tap_index in range(taps):
        running = running + joined_f[:, tap_index : tap_index + frame_span, :] * dw_weight[
            tap_index
        ].astype(jnp.float32)
    activated = jax.nn.silu(running * bn_scale + bn_shift).astype(jnp.bfloat16)

    act_all = lax.all_gather(activated, "ingest", axis=0, tiled=False)
    conv_terms = jnp.einsum(
        "grc,gcn->rn",
        act_all.reshape(groups, row_count, local_width),
        w_pw2_cols,
        preferred_element_type=jnp.float32,
    )
    residual_own = lax.dynamic_slice_in_dim(residual, me * local_width, local_width, 1)
    result = (residual_own + conv_terms).reshape(utterances, frame_span, local_width)
    live_rows = frame_index[None, :] < frames[:, None]
    layer_out = jnp.where(live_rows[:, :, None], result, 0.0).astype(jnp.bfloat16)

    keep = jnp.arange(cache_len, dtype=jnp.int32)
    kv_pick = position[None, None, :] == keep[None, :, None] + frames[:, None, None]
    kv_next = jnp.einsum(
        "srp,spd->srd", kv_pick.astype(jnp.bfloat16), memory, preferred_element_type=jnp.float32
    ).astype(jnp.bfloat16)
    conv_keep = jnp.arange(conv_len, dtype=jnp.int32)
    conv_pos = jnp.arange(joined.shape[1], dtype=jnp.int32)
    conv_pick = conv_pos[None, None, :] == conv_keep[None, :, None] + frames[:, None, None]
    conv_next = jnp.einsum(
        "srp,spd->srd", conv_pick.astype(jnp.bfloat16), joined, preferred_element_type=jnp.float32
    ).astype(jnp.bfloat16)
    return (layer_out, kv_next[:, None], conv_next)


def solution(mesh):
    in_specs = (
        P("owner", None, "ingest"),
        P("owner"),
        P("owner"),
        P("owner"),
        P("owner", "ingest", None, None),
        P("owner", None, "ingest"),
        P("owner"),
        P(),
        P(None, "ingest", None),
        P("ingest", None),
        P(),
        P(None, None, "ingest"),
        P(None, "ingest"),
        P("ingest"),
        P("ingest"),
        P("ingest", None),
    )
    out_specs = (
        P("owner", None, "ingest"),
        P("owner", "ingest", None, None),
        P("owner", None, "ingest"),
    )
    return jax.shard_map(shards, mesh=mesh, in_specs=in_specs, out_specs=out_specs, check_vma=False)
```

```python
import jax
import jax.numpy as jnp
from jax import lax
from jax.sharding import PartitionSpec as P

BLOCKS = 2


norm_eps = 1e-05


def normalize(values, gain_cols):
    model_width = values.shape[-1]
    row_mean = jnp.sum(values, axis=-1, keepdims=True) / model_width
    spread = jnp.sum(values * values, axis=-1, keepdims=True) / model_width - row_mean * row_mean
    return ((values - row_mean) * lax.rsqrt(spread + norm_eps) * gain_cols).astype(jnp.bfloat16)


def shifted_terms(block, weight_rows, groups, me):
    width = block.shape[1]
    total = jnp.dot(
        block,
        lax.dynamic_slice_in_dim(weight_rows, me * width, width, 0),
        preferred_element_type=jnp.float32,
    )
    for shift in range(1, groups):
        arrived = lax.ppermute(
            block, "ingest", perm=[(i, (i + shift) % groups) for i in range(groups)]
        )
        source = (me + groups - shift) % groups
        total = total + jnp.dot(
            arrived,
            lax.dynamic_slice_in_dim(weight_rows, source * width, width, 0),
            preferred_element_type=jnp.float32,
        )
    return total


def shards(
    frame_rows,
    route_owner,
    route_slot,
    frames,
    kv_cache,
    conv_cache,
    mig_owner,
    ln1_gain,
    w_qkv,
    w_out,
    ln2_gain,
    w_pw1,
    dw_weight,
    bn_scale,
    bn_shift,
    w_pw2,
):
    owners = lax.axis_size("owner")
    groups = lax.axis_size("ingest")
    me = lax.axis_index("ingest")
    utterances, frame_span, local_width = frame_rows.shape
    model_width = w_qkv.shape[0]
    head_dim = w_qkv.shape[2] // 3
    cache_len = kv_cache.shape[2]
    conv_len = conv_cache.shape[1]
    taps = dw_weight.shape[0]
    horizon = frame_span // BLOCKS
    moving = mig_owner.shape[0]
    settled = utterances - moving

    dest = jnp.arange(owners, dtype=jnp.int32)
    frame_pad = -(-(frame_span + 1) // 16) * 16
    slot_tag = jnp.broadcast_to(
        (route_slot + 1).astype(jnp.bfloat16)[:, None, None], (utterances, 1, local_width)
    )
    frame_rows_tagged = jnp.concatenate(
        [
            frame_rows,
            slot_tag,
            jnp.zeros((utterances, frame_pad - frame_span - 1, local_width), jnp.bfloat16),
        ],
        axis=1,
    )
    frame_send = jnp.einsum(
        "ds,stc->dtc",
        (dest[:, None] == route_owner[None, :]).astype(jnp.bfloat16),
        frame_rows_tagged,
        preferred_element_type=jnp.float32,
    ).astype(jnp.bfloat16)
    frame_got = lax.all_to_all(frame_send, "owner", split_axis=0, concat_axis=0, tiled=True)

    kv_lanes = 2 * head_dim
    conv_fold = conv_len * local_width // kv_lanes
    cache_used = cache_len + conv_fold + 1
    cache_pad = -(-cache_used // 16) * 16
    mover_tag = jnp.broadcast_to(
        (jnp.arange(moving, dtype=jnp.int32) + 1).astype(jnp.bfloat16)[:, None, None],
        (moving, 1, kv_lanes),
    )
    cache_rows = jnp.concatenate(
        [
            kv_cache[settled:, 0],
            conv_cache[settled:].reshape(moving, conv_fold, kv_lanes),
            mover_tag,
            jnp.zeros((moving, cache_pad - cache_used, kv_lanes), jnp.bfloat16),
        ],
        axis=1,
    )
    cache_send = jnp.einsum(
        "dj,jrc->drc",
        (dest[:, None] == mig_owner[None, :]).astype(jnp.bfloat16),
        cache_rows,
        preferred_element_type=jnp.float32,
    ).astype(jnp.bfloat16)
    cache_got = lax.all_to_all(cache_send, "owner", split_axis=0, concat_axis=0, tiled=True)

    got_slot = frame_got[:, frame_span, 0].astype(jnp.int32)
    slots = jnp.arange(utterances, dtype=jnp.int32)
    arranged = jnp.einsum(
        "so,otc->stc",
        (slots[:, None] + 1 == got_slot[None, :]).astype(jnp.bfloat16),
        frame_got[:, :frame_span],
        preferred_element_type=jnp.float32,
    ).astype(jnp.bfloat16)

    x_all = lax.all_gather(arranged, "ingest", axis=0, tiled=False)
    w_out_in, w_pw2_in, x_all = lax.optimization_barrier((w_out, w_pw2, x_all))
    w_out_full = lax.all_gather(w_out_in, "ingest", axis=0, tiled=True)
    w_pw2_full = lax.all_gather(w_pw2_in, "ingest", axis=0, tiled=True)
    x_rows = x_all.transpose(1, 2, 0, 3).reshape(utterances, frame_span, model_width)
    x_rows = x_rows.astype(jnp.float32)
    normed = normalize(x_rows, ln1_gain)
    projected = jnp.dot(
        normed, w_qkv.reshape(model_width, 3 * head_dim), preferred_element_type=jnp.float32
    )
    queries = projected[..., :head_dim].astype(jnp.bfloat16)
    fresh = projected[..., head_dim:].astype(jnp.bfloat16)
    w_out_full, w_pw2_full, queries, fresh = lax.optimization_barrier(
        (w_out_full, w_pw2_full, queries, fresh)
    )
    w_pw2_cols = lax.dynamic_slice_in_dim(w_pw2_full, me * local_width, local_width, 1).reshape(
        groups, local_width, local_width
    )

    got_mover = cache_got[:, cache_used - 1, 0].astype(jnp.int32)
    movers = jnp.arange(moving, dtype=jnp.int32)
    moved = jnp.einsum(
        "jo,orc->jrc",
        (movers[:, None] + 1 == got_mover[None, :]).astype(jnp.bfloat16),
        cache_got[:, : cache_used - 1],
        preferred_element_type=jnp.float32,
    ).astype(jnp.bfloat16)
    kv_state = jnp.concatenate([kv_cache[:settled, 0], moved[:, :cache_len]], axis=0)
    conv_state = jnp.concatenate(
        [conv_cache[:settled], moved[:, cache_len:].reshape(moving, conv_len, local_width)],
        axis=0,
    )

    memory = jnp.concatenate([kv_state, fresh], axis=1)
    keys_total = memory.shape[1]
    scores = jnp.einsum(
        "sqd,skd->sqk", queries, memory[..., :head_dim], preferred_element_type=jnp.float32
    ) * head_dim ** (-0.5)
    frame_index = jnp.arange(frame_span, dtype=jnp.int32)
    block_of = frame_index // horizon
    low = block_of * horizon
    high = cache_len + jnp.minimum(frames[:, None], (block_of[None, :] + 1) * horizon)
    position = jnp.arange(keys_total, dtype=jnp.int32)
    live_keys = (position[None, None, :] >= low[None, :, None]) & (
        position[None, None, :] < high[:, :, None]
    )
    scores = jnp.where(live_keys, scores, -1e30)
    row_max = jnp.max(scores, axis=-1, keepdims=True)
    weights = jnp.exp(scores - row_max)
    probabilities = (weights / jnp.sum(weights, axis=-1, keepdims=True)).astype(jnp.bfloat16)
    context = jnp.einsum(
        "sqk,skd->sqd", probabilities, memory[..., head_dim:], preferred_element_type=jnp.float32
    ).astype(jnp.bfloat16)

    row_count = utterances * frame_span
    attn = shifted_terms(context.reshape(row_count, head_dim), w_out_full, groups, me)
    residual = x_rows.reshape(row_count, model_width) + attn
    normed2 = normalize(residual, ln2_gain)
    mixed = jnp.dot(
        normed2, w_pw1.reshape(model_width, 2 * local_width), preferred_element_type=jnp.float32
    )
    glu_out = (mixed[:, :local_width] * jax.nn.sigmoid(mixed[:, local_width:])).astype(
        jnp.bfloat16
    )
    glu_out = glu_out.reshape(utterances, frame_span, local_width)

    joined = jnp.concatenate([conv_state, glu_out], axis=1)
    joined_f = joined.astype(jnp.float32)
    running = jnp.zeros((utterances, frame_span, local_width), jnp.float32)
    for tap_index in range(taps):
        running = running + joined_f[:, tap_index : tap_index + frame_span, :] * dw_weight[
            tap_index
        ].astype(jnp.float32)
    activated = jax.nn.silu(running * bn_scale + bn_shift).astype(jnp.bfloat16)

    conv_terms = shifted_terms(
        activated.reshape(row_count, local_width),
        w_pw2_cols.reshape(model_width, local_width),
        groups,
        me,
    )
    residual_own = lax.dynamic_slice_in_dim(residual, me * local_width, local_width, 1)
    result = (residual_own + conv_terms).reshape(utterances, frame_span, local_width)
    live_rows = frame_index[None, :] < frames[:, None]
    layer_out = jnp.where(live_rows[:, :, None], result, 0.0).astype(jnp.bfloat16)

    keep = jnp.arange(cache_len, dtype=jnp.int32)
    kv_pick = position[None, None, :] == keep[None, :, None] + frames[:, None, None]
    kv_next = jnp.einsum(
        "srp,spd->srd", kv_pick.astype(jnp.bfloat16), memory, preferred_element_type=jnp.float32
    ).astype(jnp.bfloat16)
    conv_keep = jnp.arange(conv_len, dtype=jnp.int32)
    conv_pos = jnp.arange(joined.shape[1], dtype=jnp.int32)
    conv_pick = conv_pos[None, None, :] == conv_keep[None, :, None] + frames[:, None, None]
    conv_next = jnp.einsum(
        "srp,spd->srd", conv_pick.astype(jnp.bfloat16), joined, preferred_element_type=jnp.float32
    ).astype(jnp.bfloat16)
    return (layer_out, kv_next.reshape(kv_cache.shape), conv_next)


def solution(mesh):
    in_specs = (
        P("owner", None, "ingest"),
        P("owner"),
        P("owner"),
        P("owner"),
        P("owner", "ingest", None, None),
        P("owner", None, "ingest"),
        P("owner"),
        P(),
        P(None, "ingest", None),
        P("ingest", None),
        P(),
        P(None, None, "ingest"),
        P(None, "ingest"),
        P("ingest"),
        P("ingest"),
        P("ingest", None),
    )
    out_specs = (
        P("owner", None, "ingest"),
        P("owner", "ingest", None, None),
        P("owner", None, "ingest"),
    )
    return jax.shard_map(shards, mesh=mesh, in_specs=in_specs, out_specs=out_specs, check_vma=False)
```

```python
import jax
import jax.numpy as jnp
from jax import lax
from jax.sharding import PartitionSpec as P

BLOCKS = 2


norm_eps = 1e-05


def normalize(values, gain_cols):
    model_width = values.shape[-1]
    row_mean = jnp.sum(values, axis=-1, keepdims=True) / model_width
    spread = jnp.sum(values * values, axis=-1, keepdims=True) / model_width - row_mean * row_mean
    return ((values - row_mean) * lax.rsqrt(spread + norm_eps) * gain_cols).astype(jnp.bfloat16)


def shards(
    frame_rows,
    route_owner,
    route_slot,
    frames,
    kv_cache,
    conv_cache,
    mig_owner,
    ln1_gain,
    w_qkv,
    w_out,
    ln2_gain,
    w_pw1,
    dw_weight,
    bn_scale,
    bn_shift,
    w_pw2,
):
    owners = lax.axis_size("owner")
    groups = lax.axis_size("ingest")
    me = lax.axis_index("ingest")
    utterances, frame_span, local_width = frame_rows.shape
    model_width = w_qkv.shape[0]
    head_dim = w_qkv.shape[2] // 3
    cache_len = kv_cache.shape[2]
    conv_len = conv_cache.shape[1]
    taps = dw_weight.shape[0]
    horizon = frame_span // BLOCKS
    moving = mig_owner.shape[0]
    settled = utterances - moving

    dest = jnp.arange(owners, dtype=jnp.int32)
    frame_pad = -(-(frame_span + 1) // 16) * 16
    slot_tag = jnp.broadcast_to(
        (route_slot + 1).astype(jnp.bfloat16)[:, None, None], (utterances, 1, local_width)
    )
    frame_rows_tagged = jnp.concatenate(
        [
            frame_rows,
            slot_tag,
            jnp.zeros((utterances, frame_pad - frame_span - 1, local_width), jnp.bfloat16),
        ],
        axis=1,
    )
    frame_send = jnp.einsum(
        "ds,stc->dtc",
        (dest[:, None] == route_owner[None, :]).astype(jnp.bfloat16),
        frame_rows_tagged,
        preferred_element_type=jnp.float32,
    ).astype(jnp.bfloat16)

    kv_lanes = 2 * head_dim
    conv_fold = conv_len * local_width // kv_lanes
    cache_used = cache_len + conv_fold + 1
    cache_pad = -(-cache_used // 16) * 16
    mover_tag = jnp.broadcast_to(
        (jnp.arange(moving, dtype=jnp.int32) + 1).astype(jnp.bfloat16)[:, None, None],
        (moving, 1, kv_lanes),
    )
    cache_rows = jnp.concatenate(
        [
            kv_cache[settled:, 0],
            conv_cache[settled:].reshape(moving, conv_fold, kv_lanes),
            mover_tag,
            jnp.zeros((moving, cache_pad - cache_used, kv_lanes), jnp.bfloat16),
        ],
        axis=1,
    )
    cache_send = jnp.einsum(
        "dj,jrc->drc",
        (dest[:, None] == mig_owner[None, :]).astype(jnp.bfloat16),
        cache_rows,
        preferred_element_type=jnp.float32,
    ).astype(jnp.bfloat16)
    frame_send = frame_send + 0 * cache_send[:, : frame_send.shape[1], : frame_send.shape[2]]
    frame_got = lax.all_to_all(frame_send, "owner", split_axis=0, concat_axis=0, tiled=True)
    cache_got = lax.all_to_all(cache_send, "owner", split_axis=0, concat_axis=0, tiled=True)

    got_slot = frame_got[:, frame_span, 0].astype(jnp.int32)
    slots = jnp.arange(utterances, dtype=jnp.int32)
    arranged = jnp.einsum(
        "so,otc->stc",
        (slots[:, None] + 1 == got_slot[None, :]).astype(jnp.bfloat16),
        frame_got[:, :frame_span],
        preferred_element_type=jnp.float32,
    ).astype(jnp.bfloat16)

    x_all = lax.all_gather(arranged, "ingest", axis=0, tiled=False)
    w_out_in, w_pw2_in, x_all = lax.optimization_barrier((w_out, w_pw2, x_all))
    w_out_full = lax.all_gather(w_out_in, "ingest", axis=0, tiled=True)
    w_pw2_full = lax.all_gather(w_pw2_in, "ingest", axis=0, tiled=True)
    x_plain = x_all.transpose(1, 2, 0, 3).reshape(utterances, frame_span, model_width)
    normed = normalize(x_plain.astype(jnp.float32), ln1_gain)
    projected = jnp.dot(
        normed, w_qkv.reshape(model_width, 3 * head_dim), preferred_element_type=jnp.float32
    )
    queries = projected[..., :head_dim].astype(jnp.bfloat16)
    fresh = projected[..., head_dim:].astype(jnp.bfloat16)
    w_out_full, w_pw2_full, x_plain, queries, fresh = lax.optimization_barrier(
        (w_out_full, w_pw2_full, x_plain, queries, fresh)
    )
    w_pw2_cols = lax.dynamic_slice_in_dim(w_pw2_full, me * local_width, local_width, 1).reshape(
        groups, local_width, local_width
    )

    got_mover = cache_got[:, cache_used - 1, 0].astype(jnp.int32)
    movers = jnp.arange(moving, dtype=jnp.int32)
    moved = jnp.einsum(
        "jo,orc->jrc",
        (movers[:, None] + 1 == got_mover[None, :]).astype(jnp.bfloat16),
        cache_got[:, : cache_used - 1],
        preferred_element_type=jnp.float32,
    ).astype(jnp.bfloat16)
    kv_state = jnp.concatenate([kv_cache[:settled, 0], moved[:, :cache_len]], axis=0)
    conv_state = jnp.concatenate(
        [conv_cache[:settled], moved[:, cache_len:].reshape(moving, conv_len, local_width)],
        axis=0,
    )

    memory = jnp.concatenate([kv_state, fresh], axis=1)
    keys_total = memory.shape[1]
    scores = jnp.einsum(
        "sqd,skd->sqk", queries, memory[..., :head_dim], preferred_element_type=jnp.float32
    ) * head_dim ** (-0.5)
    frame_index = jnp.arange(frame_span, dtype=jnp.int32)
    block_of = frame_index // horizon
    low = block_of * horizon
    high = cache_len + jnp.minimum(frames[:, None], (block_of[None, :] + 1) * horizon)
    position = jnp.arange(keys_total, dtype=jnp.int32)
    live_keys = (position[None, None, :] >= low[None, :, None]) & (
        position[None, None, :] < high[:, :, None]
    )
    scores = jnp.where(live_keys, scores, -1e30)
    row_max = jnp.max(scores, axis=-1, keepdims=True)
    weights = jnp.exp(scores - row_max)
    probabilities = (weights / jnp.sum(weights, axis=-1, keepdims=True)).astype(jnp.bfloat16)
    context = jnp.einsum(
        "sqk,skd->sqd", probabilities, memory[..., head_dim:], preferred_element_type=jnp.float32
    ).astype(jnp.bfloat16)

    ctx_all = lax.all_gather(context, "ingest", axis=0, tiled=False)
    row_count = utterances * frame_span
    attn = jnp.einsum(
        "grc,gcn->rn",
        ctx_all.reshape(groups, row_count, head_dim),
        w_out_full.reshape(groups, head_dim, model_width),
        preferred_element_type=jnp.float32,
    )
    residual = x_plain.reshape(row_count, model_width).astype(jnp.float32) + attn
    normed2 = normalize(residual, ln2_gain)
    mixed = jnp.dot(
        normed2, w_pw1.reshape(model_width, 2 * local_width), preferred_element_type=jnp.float32
    )
    glu_out = (mixed[:, :local_width] * jax.nn.sigmoid(mixed[:, local_width:])).astype(
        jnp.bfloat16
    )
    glu_out = glu_out.reshape(utterances, frame_span, local_width)

    joined = jnp.concatenate([conv_state, glu_out], axis=1)
    joined_f = joined.astype(jnp.float32)
    running = jnp.zeros((utterances, frame_span, local_width), jnp.float32)
    for tap_index in range(taps):
        running = running + joined_f[:, tap_index : tap_index + frame_span, :] * dw_weight[
            tap_index
        ].astype(jnp.float32)
    activated = jax.nn.silu(running * bn_scale + bn_shift).astype(jnp.bfloat16)

    act_all = lax.all_gather(activated, "ingest", axis=0, tiled=False)
    conv_terms = jnp.einsum(
        "grc,gcn->rn",
        act_all.reshape(groups, row_count, local_width),
        w_pw2_cols,
        preferred_element_type=jnp.float32,
    )
    residual_own = lax.dynamic_slice_in_dim(residual, me * local_width, local_width, 1)
    result = (residual_own + conv_terms).reshape(utterances, frame_span, local_width)
    live_rows = frame_index[None, :] < frames[:, None]
    layer_out = jnp.where(live_rows[:, :, None], result, 0.0).astype(jnp.bfloat16)

    keep = jnp.arange(cache_len, dtype=jnp.int32)
    kv_pick = position[None, None, :] == keep[None, :, None] + frames[:, None, None]
    kv_next = jnp.einsum(
        "srp,spd->srd", kv_pick.astype(jnp.bfloat16), memory, preferred_element_type=jnp.float32
    ).astype(jnp.bfloat16)
    conv_keep = jnp.arange(conv_len, dtype=jnp.int32)
    conv_pos = jnp.arange(joined.shape[1], dtype=jnp.int32)
    conv_pick = conv_pos[None, None, :] == conv_keep[None, :, None] + frames[:, None, None]
    conv_next = jnp.einsum(
        "srp,spd->srd", conv_pick.astype(jnp.bfloat16), joined, preferred_element_type=jnp.float32
    ).astype(jnp.bfloat16)
    return (layer_out, kv_next.reshape(kv_cache.shape), conv_next)


def solution(mesh):
    in_specs = (
        P("owner", None, "ingest"),
        P("owner"),
        P("owner"),
        P("owner"),
        P("owner", "ingest", None, None),
        P("owner", None, "ingest"),
        P("owner"),
        P(),
        P(None, "ingest", None),
        P("ingest", None),
        P(),
        P(None, None, "ingest"),
        P(None, "ingest"),
        P("ingest"),
        P("ingest"),
        P("ingest", None),
    )
    out_specs = (
        P("owner", None, "ingest"),
        P("owner", "ingest", None, None),
        P("owner", None, "ingest"),
    )
    return jax.shard_map(shards, mesh=mesh, in_specs=in_specs, out_specs=out_specs, check_vma=False)
```

```python
import jax
import jax.numpy as jnp
from jax import lax
from jax.sharding import PartitionSpec as P

BLOCKS = 2


norm_eps = 1e-05


def normalize(values, gain_cols):
    model_width = values.shape[-1]
    row_mean = jnp.sum(values, axis=-1, keepdims=True) / model_width
    spread = jnp.sum(values * values, axis=-1, keepdims=True) / model_width - row_mean * row_mean
    return ((values - row_mean) * lax.rsqrt(spread + norm_eps) * gain_cols).astype(jnp.bfloat16)


def shards(
    frame_rows,
    route_owner,
    route_slot,
    frames,
    kv_cache,
    conv_cache,
    mig_owner,
    ln1_gain,
    w_qkv,
    w_out,
    ln2_gain,
    w_pw1,
    dw_weight,
    bn_scale,
    bn_shift,
    w_pw2,
):
    owners = lax.axis_size("owner")
    groups = lax.axis_size("ingest")
    me = lax.axis_index("ingest")
    utterances, frame_span, local_width = frame_rows.shape
    model_width = w_qkv.shape[0]
    head_dim = w_qkv.shape[2] // 3
    cache_len = kv_cache.shape[2]
    conv_len = conv_cache.shape[1]
    taps = dw_weight.shape[0]
    horizon = frame_span // BLOCKS
    moving = mig_owner.shape[0]
    settled = utterances - moving

    dest = jnp.arange(owners, dtype=jnp.int32)
    frame_pad = -(-(frame_span + 1) // 16) * 16
    slot_tag = jnp.broadcast_to(
        (route_slot + 1).astype(jnp.bfloat16)[:, None, None], (utterances, 1, local_width)
    )
    frame_rows_tagged = jnp.concatenate(
        [
            frame_rows,
            slot_tag,
            jnp.zeros((utterances, frame_pad - frame_span - 1, local_width), jnp.bfloat16),
        ],
        axis=1,
    )
    frame_send = jnp.einsum(
        "ds,stc->dtc",
        (dest[:, None] == route_owner[None, :]).astype(jnp.bfloat16),
        frame_rows_tagged,
        preferred_element_type=jnp.float32,
    ).astype(jnp.bfloat16)
    frame_got = lax.all_to_all(frame_send, "owner", split_axis=0, concat_axis=0, tiled=True)

    kv_lanes = 2 * head_dim
    conv_fold = conv_len * local_width // kv_lanes
    cache_used = cache_len + conv_fold + 1
    cache_pad = -(-cache_used // 16) * 16
    mover_tag = jnp.broadcast_to(
        (jnp.arange(moving, dtype=jnp.int32) + 1).astype(jnp.bfloat16)[:, None, None],
        (moving, 1, kv_lanes),
    )
    cache_rows = jnp.concatenate(
        [
            kv_cache[settled:, 0],
            conv_cache[settled:].reshape(moving, conv_fold, kv_lanes),
            mover_tag,
            jnp.zeros((moving, cache_pad - cache_used, kv_lanes), jnp.bfloat16),
        ],
        axis=1,
    )
    cache_send = jnp.einsum(
        "dj,jrc->drc",
        (dest[:, None] == mig_owner[None, :]).astype(jnp.bfloat16),
        cache_rows,
        preferred_element_type=jnp.float32,
    ).astype(jnp.bfloat16)
    cache_got = lax.all_to_all(cache_send, "owner", split_axis=0, concat_axis=0, tiled=True)

    got_slot = frame_got[:, frame_span, 0].astype(jnp.int32)
    slots = jnp.arange(utterances, dtype=jnp.int32)
    arranged = jnp.einsum(
        "so,otc->stc",
        (slots[:, None] + 1 == got_slot[None, :]).astype(jnp.bfloat16),
        frame_got[:, :frame_span],
        preferred_element_type=jnp.float32,
    ).astype(jnp.bfloat16)

    out_span = frame_span
    frame_span = -(-frame_span // 16) * 16
    arranged = jnp.pad(arranged, ((0, 0), (0, frame_span - out_span), (0, 0)))

    x_all = lax.all_gather(arranged, "ingest", axis=0, tiled=False)
    w_out_in, w_pw2_in, x_all = lax.optimization_barrier((w_out, w_pw2, x_all))
    w_out_full = lax.all_gather(w_out_in, "ingest", axis=0, tiled=True)
    w_pw2_full = lax.all_gather(w_pw2_in, "ingest", axis=0, tiled=True)
    x_rows = x_all.transpose(1, 2, 0, 3).reshape(utterances, frame_span, model_width)
    x_rows = x_rows.astype(jnp.float32)
    normed = normalize(x_rows, ln1_gain)
    projected = jnp.dot(
        normed, w_qkv.reshape(model_width, 3 * head_dim), preferred_element_type=jnp.float32
    )
    queries = projected[..., :head_dim].astype(jnp.bfloat16)
    fresh = projected[..., head_dim:].astype(jnp.bfloat16)
    w_out_full, w_pw2_full, queries, fresh = lax.optimization_barrier(
        (w_out_full, w_pw2_full, queries, fresh)
    )
    w_pw2_cols = lax.dynamic_slice_in_dim(w_pw2_full, me * local_width, local_width, 1).reshape(
        groups, local_width, local_width
    )

    got_mover = cache_got[:, cache_used - 1, 0].astype(jnp.int32)
    movers = jnp.arange(moving, dtype=jnp.int32)
    moved = jnp.einsum(
        "jo,orc->jrc",
        (movers[:, None] + 1 == got_mover[None, :]).astype(jnp.bfloat16),
        cache_got[:, : cache_used - 1],
        preferred_element_type=jnp.float32,
    ).astype(jnp.bfloat16)
    kv_state = jnp.concatenate([kv_cache[:settled, 0], moved[:, :cache_len]], axis=0)
    conv_state = jnp.concatenate(
        [conv_cache[:settled], moved[:, cache_len:].reshape(moving, conv_len, local_width)],
        axis=0,
    )

    memory = jnp.concatenate([kv_state, fresh], axis=1)
    keys_total = memory.shape[1]
    scores = jnp.einsum(
        "sqd,skd->sqk", queries, memory[..., :head_dim], preferred_element_type=jnp.float32
    ) * head_dim ** (-0.5)
    frame_index = jnp.arange(frame_span, dtype=jnp.int32)
    block_of = frame_index // horizon
    low = block_of * horizon
    high = cache_len + jnp.minimum(frames[:, None], (block_of[None, :] + 1) * horizon)
    position = jnp.arange(keys_total, dtype=jnp.int32)
    live_keys = (position[None, None, :] >= low[None, :, None]) & (
        position[None, None, :] < high[:, :, None]
    )
    scores = jnp.where(live_keys, scores, -1e30)
    row_max = jnp.max(scores, axis=-1, keepdims=True)
    weights = jnp.exp(scores - row_max)
    probabilities = (weights / jnp.sum(weights, axis=-1, keepdims=True)).astype(jnp.bfloat16)
    context = jnp.einsum(
        "sqk,skd->sqd", probabilities, memory[..., head_dim:], preferred_element_type=jnp.float32
    ).astype(jnp.bfloat16)

    ctx_all = lax.all_gather(context, "ingest", axis=0, tiled=False)
    row_count = utterances * frame_span
    attn = jnp.einsum(
        "grc,gcn->rn",
        ctx_all.reshape(groups, row_count, head_dim),
        w_out_full.reshape(groups, head_dim, model_width),
        preferred_element_type=jnp.float32,
    )
    residual = x_rows.reshape(row_count, model_width) + attn
    normed2 = normalize(residual, ln2_gain)
    mixed = jnp.dot(
        normed2, w_pw1.reshape(model_width, 2 * local_width), preferred_element_type=jnp.float32
    )
    glu_out = (mixed[:, :local_width] * jax.nn.sigmoid(mixed[:, local_width:])).astype(
        jnp.bfloat16
    )
    glu_out = glu_out.reshape(utterances, frame_span, local_width)

    joined = jnp.concatenate([conv_state, glu_out], axis=1)
    joined_f = joined.astype(jnp.float32)
    running = jnp.zeros((utterances, frame_span, local_width), jnp.float32)
    for tap_index in range(taps):
        running = running + joined_f[:, tap_index : tap_index + frame_span, :] * dw_weight[
            tap_index
        ].astype(jnp.float32)
    activated = jax.nn.silu(running * bn_scale + bn_shift).astype(jnp.bfloat16)

    act_all = lax.all_gather(activated, "ingest", axis=0, tiled=False)
    conv_terms = jnp.einsum(
        "grc,gcn->rn",
        act_all.reshape(groups, row_count, local_width),
        w_pw2_cols,
        preferred_element_type=jnp.float32,
    )
    residual_own = lax.dynamic_slice_in_dim(residual, me * local_width, local_width, 1)
    result = (residual_own + conv_terms).reshape(utterances, frame_span, local_width)
    live_rows = frame_index[None, :] < frames[:, None]
    layer_out = jnp.where(live_rows[:, :, None], result, 0.0).astype(jnp.bfloat16)
    layer_out = layer_out[:, :out_span]

    keep = jnp.arange(cache_len, dtype=jnp.int32)
    kv_pick = position[None, None, :] == keep[None, :, None] + frames[:, None, None]
    kv_next = jnp.einsum(
        "srp,spd->srd", kv_pick.astype(jnp.bfloat16), memory, preferred_element_type=jnp.float32
    ).astype(jnp.bfloat16)
    conv_keep = jnp.arange(conv_len, dtype=jnp.int32)
    conv_pos = jnp.arange(joined.shape[1], dtype=jnp.int32)
    conv_pick = conv_pos[None, None, :] == conv_keep[None, :, None] + frames[:, None, None]
    conv_next = jnp.einsum(
        "srp,spd->srd", conv_pick.astype(jnp.bfloat16), joined, preferred_element_type=jnp.float32
    ).astype(jnp.bfloat16)
    return (layer_out, kv_next.reshape(kv_cache.shape), conv_next)


def solution(mesh):
    in_specs = (
        P("owner", None, "ingest"),
        P("owner"),
        P("owner"),
        P("owner"),
        P("owner", "ingest", None, None),
        P("owner", None, "ingest"),
        P("owner"),
        P(),
        P(None, "ingest", None),
        P("ingest", None),
        P(),
        P(None, None, "ingest"),
        P(None, "ingest"),
        P("ingest"),
        P("ingest"),
        P("ingest", None),
    )
    out_specs = (
        P("owner", None, "ingest"),
        P("owner", "ingest", None, None),
        P("owner", None, "ingest"),
    )
    return jax.shard_map(shards, mesh=mesh, in_specs=in_specs, out_specs=out_specs, check_vma=False)
```

```python
import jax
import jax.numpy as jnp
from jax import lax
from jax.sharding import PartitionSpec as P

BLOCKS = 2


norm_eps = 1e-05


def normalize(values, gain_cols):
    model_width = values.shape[-1]
    row_mean = jnp.sum(values, axis=-1, keepdims=True) / model_width
    spread = jnp.sum(values * values, axis=-1, keepdims=True) / model_width - row_mean * row_mean
    return ((values - row_mean) * lax.rsqrt(spread + norm_eps) * gain_cols).astype(jnp.bfloat16)


def shards(
    frame_rows,
    route_owner,
    route_slot,
    frames,
    kv_cache,
    conv_cache,
    mig_owner,
    ln1_gain,
    w_qkv,
    w_out,
    ln2_gain,
    w_pw1,
    dw_weight,
    bn_scale,
    bn_shift,
    w_pw2,
):
    owners = lax.axis_size("owner")
    groups = lax.axis_size("ingest")
    me = lax.axis_index("ingest")
    utterances, frame_span, local_width = frame_rows.shape
    model_width = w_qkv.shape[0]
    head_dim = w_qkv.shape[2] // 3
    cache_len = kv_cache.shape[2]
    conv_len = conv_cache.shape[1]
    taps = dw_weight.shape[0]
    horizon = frame_span // BLOCKS
    moving = mig_owner.shape[0]
    settled = utterances - moving

    dest = jnp.arange(owners, dtype=jnp.int32)
    frame_pad = -(-(frame_span + 1) // 16) * 16
    slot_tag = jnp.broadcast_to(
        (route_slot + 1).astype(jnp.bfloat16)[:, None, None], (utterances, 1, local_width)
    )
    frame_rows_tagged = jnp.concatenate(
        [
            frame_rows,
            slot_tag,
            jnp.zeros((utterances, frame_pad - frame_span - 1, local_width), jnp.bfloat16),
        ],
        axis=1,
    )
    frame_send = jnp.einsum(
        "ds,stc->dtc",
        (dest[:, None] == route_owner[None, :]).astype(jnp.bfloat16),
        frame_rows_tagged,
        preferred_element_type=jnp.float32,
    ).astype(jnp.bfloat16)
    frame_got = lax.all_to_all(frame_send, "owner", split_axis=0, concat_axis=0, tiled=True)

    kv_lanes = 2 * head_dim
    conv_fold = conv_len * local_width // kv_lanes
    cache_used = cache_len + conv_fold + 1
    cache_pad = -(-cache_used // 16) * 16
    mover_tag = jnp.broadcast_to(
        (jnp.arange(moving, dtype=jnp.int32) + 1).astype(jnp.bfloat16)[:, None, None],
        (moving, 1, kv_lanes),
    )
    cache_rows = jnp.concatenate(
        [
            kv_cache[settled:, 0],
            conv_cache[settled:].reshape(moving, conv_fold, kv_lanes),
            mover_tag,
            jnp.zeros((moving, cache_pad - cache_used, kv_lanes), jnp.bfloat16),
        ],
        axis=1,
    )
    cache_send = jnp.einsum(
        "dj,jrc->drc",
        (dest[:, None] == mig_owner[None, :]).astype(jnp.bfloat16),
        cache_rows,
        preferred_element_type=jnp.float32,
    ).astype(jnp.bfloat16)
    cache_got = lax.all_to_all(cache_send, "owner", split_axis=0, concat_axis=0, tiled=True)

    got_slot = frame_got[:, frame_span, 0].astype(jnp.int32)
    slots = jnp.arange(utterances, dtype=jnp.int32)
    arranged = jnp.einsum(
        "so,otc->stc",
        (slots[:, None] + 1 == got_slot[None, :]).astype(jnp.bfloat16),
        frame_got[:, :frame_span],
        preferred_element_type=jnp.float32,
    ).astype(jnp.bfloat16)

    out_span = frame_span
    frame_span = -(-frame_span // 16) * 16
    arranged = jnp.pad(arranged, ((0, 0), (0, frame_span - out_span), (0, 0)))

    x_all = lax.all_gather(arranged, "ingest", axis=0, tiled=False)
    w_out_in, w_pw2_in, x_all = lax.optimization_barrier((w_out, w_pw2, x_all))
    w_out_full = lax.all_gather(w_out_in, "ingest", axis=0, tiled=True)
    w_pw2_full = lax.all_gather(w_pw2_in, "ingest", axis=0, tiled=True)
    x_plain = x_all.transpose(1, 2, 0, 3).reshape(utterances, frame_span, model_width)
    normed = normalize(x_plain.astype(jnp.float32), ln1_gain)
    projected = jnp.dot(
        normed, w_qkv.reshape(model_width, 3 * head_dim), preferred_element_type=jnp.float32
    )
    queries = projected[..., :head_dim].astype(jnp.bfloat16)
    fresh = projected[..., head_dim:].astype(jnp.bfloat16)
    w_out_full, w_pw2_full, x_plain, queries, fresh = lax.optimization_barrier(
        (w_out_full, w_pw2_full, x_plain, queries, fresh)
    )
    w_pw2_cols = lax.dynamic_slice_in_dim(w_pw2_full, me * local_width, local_width, 1).reshape(
        groups, local_width, local_width
    )

    got_mover = cache_got[:, cache_used - 1, 0].astype(jnp.int32)
    movers = jnp.arange(moving, dtype=jnp.int32)
    moved = jnp.einsum(
        "jo,orc->jrc",
        (movers[:, None] + 1 == got_mover[None, :]).astype(jnp.bfloat16),
        cache_got[:, : cache_used - 1],
        preferred_element_type=jnp.float32,
    ).astype(jnp.bfloat16)
    kv_state = jnp.concatenate([kv_cache[:settled, 0], moved[:, :cache_len]], axis=0)
    conv_state = jnp.concatenate(
        [conv_cache[:settled], moved[:, cache_len:].reshape(moving, conv_len, local_width)],
        axis=0,
    )

    memory = jnp.concatenate([kv_state, fresh], axis=1)
    keys_total = memory.shape[1]
    scores = jnp.einsum(
        "sqd,skd->sqk", queries, memory[..., :head_dim], preferred_element_type=jnp.float32
    ) * head_dim ** (-0.5)
    frame_index = jnp.arange(frame_span, dtype=jnp.int32)
    block_of = frame_index // horizon
    low = block_of * horizon
    high = cache_len + jnp.minimum(frames[:, None], (block_of[None, :] + 1) * horizon)
    position = jnp.arange(keys_total, dtype=jnp.int32)
    live_keys = (position[None, None, :] >= low[None, :, None]) & (
        position[None, None, :] < high[:, :, None]
    )
    scores = jnp.where(live_keys, scores, -1e30)
    row_max = jnp.max(scores, axis=-1, keepdims=True)
    weights = jnp.exp(scores - row_max)
    probabilities = (weights / jnp.sum(weights, axis=-1, keepdims=True)).astype(jnp.bfloat16)
    context = jnp.einsum(
        "sqk,skd->sqd", probabilities, memory[..., head_dim:], preferred_element_type=jnp.float32
    ).astype(jnp.bfloat16)

    ctx_all = lax.all_gather(context, "ingest", axis=0, tiled=False)
    row_count = utterances * frame_span
    attn = jnp.einsum(
        "grc,gcn->rn",
        ctx_all.reshape(groups, row_count, head_dim),
        w_out_full.reshape(groups, head_dim, model_width),
        preferred_element_type=jnp.float32,
    )
    residual = x_plain.reshape(row_count, model_width).astype(jnp.float32) + attn
    normed2 = normalize(residual, ln2_gain)
    mixed = jnp.dot(
        normed2, w_pw1.reshape(model_width, 2 * local_width), preferred_element_type=jnp.float32
    )
    glu_out = (mixed[:, :local_width] * jax.nn.sigmoid(mixed[:, local_width:])).astype(
        jnp.bfloat16
    )
    glu_out = glu_out.reshape(utterances, frame_span, local_width)

    joined = jnp.concatenate([conv_state, glu_out], axis=1)
    joined_f = joined.astype(jnp.float32)
    running = jnp.zeros((utterances, frame_span, local_width), jnp.float32)
    for tap_index in range(taps):
        running = running + joined_f[:, tap_index : tap_index + frame_span, :] * dw_weight[
            tap_index
        ].astype(jnp.float32)
    activated = jax.nn.silu(running * bn_scale + bn_shift).astype(jnp.bfloat16)

    act_all = lax.all_gather(activated, "ingest", axis=0, tiled=False)
    conv_terms = jnp.einsum(
        "grc,gcn->rn",
        act_all.reshape(groups, row_count, local_width),
        w_pw2_cols,
        preferred_element_type=jnp.float32,
    )
    residual_own = lax.dynamic_slice_in_dim(residual, me * local_width, local_width, 1)
    result = (residual_own + conv_terms).reshape(utterances, frame_span, local_width)
    live_rows = frame_index[None, :] < frames[:, None]
    layer_out = jnp.where(live_rows[:, :, None], result, 0.0).astype(jnp.bfloat16)
    layer_out = layer_out[:, :out_span]

    keep = jnp.arange(cache_len, dtype=jnp.int32)
    kv_pick = position[None, None, :] == keep[None, :, None] + frames[:, None, None]
    kv_next = jnp.einsum(
        "srp,spd->srd", kv_pick.astype(jnp.bfloat16), memory, preferred_element_type=jnp.float32
    ).astype(jnp.bfloat16)
    conv_keep = jnp.arange(conv_len, dtype=jnp.int32)
    conv_pos = jnp.arange(joined.shape[1], dtype=jnp.int32)
    conv_pick = conv_pos[None, None, :] == conv_keep[None, :, None] + frames[:, None, None]
    conv_next = jnp.einsum(
        "srp,spd->srd", conv_pick.astype(jnp.bfloat16), joined, preferred_element_type=jnp.float32
    ).astype(jnp.bfloat16)
    return (layer_out, kv_next.reshape(kv_cache.shape), conv_next)


def solution(mesh):
    in_specs = (
        P("owner", None, "ingest"),
        P("owner"),
        P("owner"),
        P("owner"),
        P("owner", "ingest", None, None),
        P("owner", None, "ingest"),
        P("owner"),
        P(),
        P(None, "ingest", None),
        P("ingest", None),
        P(),
        P(None, None, "ingest"),
        P(None, "ingest"),
        P("ingest"),
        P("ingest"),
        P("ingest", None),
    )
    out_specs = (
        P("owner", None, "ingest"),
        P("owner", "ingest", None, None),
        P("owner", None, "ingest"),
    )
    return jax.shard_map(shards, mesh=mesh, in_specs=in_specs, out_specs=out_specs, check_vma=False)
```

```python
import jax
import jax.numpy as jnp
from jax import lax
from jax.sharding import PartitionSpec as P

BLOCKS = 2


norm_eps = 1e-05


def normalize(values, gain_cols):
    model_width = values.shape[-1]
    row_mean = jnp.sum(values, axis=-1, keepdims=True) / model_width
    spread = jnp.sum(values * values, axis=-1, keepdims=True) / model_width - row_mean * row_mean
    return ((values - row_mean) * lax.rsqrt(spread + norm_eps) * gain_cols).astype(jnp.bfloat16)


def shards(
    frame_rows,
    route_owner,
    route_slot,
    frames,
    kv_cache,
    conv_cache,
    mig_owner,
    ln1_gain,
    w_qkv,
    w_out,
    ln2_gain,
    w_pw1,
    dw_weight,
    bn_scale,
    bn_shift,
    w_pw2,
):
    owners = lax.axis_size("owner")
    groups = lax.axis_size("ingest")
    me = lax.axis_index("ingest")
    utterances, frame_span, local_width = frame_rows.shape
    model_width = w_qkv.shape[0]
    head_dim = w_qkv.shape[2] // 3
    cache_len = kv_cache.shape[2]
    conv_len = conv_cache.shape[1]
    taps = dw_weight.shape[0]
    horizon = frame_span // BLOCKS
    moving = mig_owner.shape[0]
    settled = utterances - moving

    dest = jnp.arange(owners, dtype=jnp.int32)
    frame_pad = -(-(frame_span + conv_len + 2) // 16) * 16
    slot_tag = jnp.broadcast_to(
        (route_slot + 1).astype(jnp.bfloat16)[:, None, None], (utterances, 1, local_width)
    )
    frame_send = jnp.einsum(
        "ds,stc->dtc",
        (dest[:, None] == route_owner[None, :]).astype(jnp.bfloat16),
        jnp.concatenate([frame_rows, slot_tag], axis=1),
        preferred_element_type=jnp.float32,
    ).astype(jnp.bfloat16)
    mover_tag = jnp.broadcast_to(
        (jnp.arange(moving, dtype=jnp.int32) + 1).astype(jnp.bfloat16)[:, None, None],
        (moving, 1, local_width),
    )
    mig_pick = (dest[:, None] == mig_owner[None, :]).astype(jnp.bfloat16)
    conv_send = jnp.einsum(
        "dj,jrc->drc",
        mig_pick,
        jnp.concatenate([conv_cache[settled:], mover_tag], axis=1),
        preferred_element_type=jnp.float32,
    ).astype(jnp.bfloat16)
    frame_send = jnp.concatenate(
        [
            frame_send,
            conv_send,
            jnp.zeros((owners, frame_pad - frame_span - conv_len - 2, local_width), jnp.bfloat16),
        ],
        axis=1,
    )
    frame_got = lax.all_to_all(frame_send, "owner", split_axis=0, concat_axis=0, tiled=True)

    kv_lanes = 2 * head_dim
    kv_rows = cache_len * kv_lanes // local_width
    cache_pad = -(-kv_rows // 16) * 16
    cache_rows = jnp.concatenate(
        [
            kv_cache[settled:, 0].reshape(moving, kv_rows, local_width),
            jnp.zeros((moving, cache_pad - kv_rows, local_width), jnp.bfloat16),
        ],
        axis=1,
    )
    cache_send = jnp.einsum(
        "dj,jrc->drc", mig_pick, cache_rows, preferred_element_type=jnp.float32
    ).astype(jnp.bfloat16)
    cache_got = lax.all_to_all(cache_send, "owner", split_axis=0, concat_axis=0, tiled=True)

    got_slot = frame_got[:, frame_span, 0].astype(jnp.int32)
    slots = jnp.arange(utterances, dtype=jnp.int32)
    arranged = jnp.einsum(
        "so,otc->stc",
        (slots[:, None] + 1 == got_slot[None, :]).astype(jnp.bfloat16),
        frame_got[:, :frame_span],
        preferred_element_type=jnp.float32,
    ).astype(jnp.bfloat16)

    out_span = frame_span
    frame_span = -(-frame_span // 16) * 16
    arranged = jnp.pad(arranged, ((0, 0), (0, frame_span - out_span), (0, 0)))

    x_all = lax.all_gather(arranged, "ingest", axis=0, tiled=False)
    w_out_in, w_pw2_in, x_all = lax.optimization_barrier((w_out, w_pw2, x_all))
    w_out_full = lax.all_gather(w_out_in, "ingest", axis=0, tiled=True)
    w_pw2_full = lax.all_gather(w_pw2_in, "ingest", axis=0, tiled=True)
    x_rows = x_all.transpose(1, 2, 0, 3).reshape(utterances, frame_span, model_width)
    x_rows = x_rows.astype(jnp.float32)
    normed = normalize(x_rows, ln1_gain)
    projected = jnp.dot(
        normed, w_qkv.reshape(model_width, 3 * head_dim), preferred_element_type=jnp.float32
    )
    queries = projected[..., :head_dim].astype(jnp.bfloat16)
    fresh = projected[..., head_dim:].astype(jnp.bfloat16)
    w_out_full, w_pw2_full, queries, fresh = lax.optimization_barrier(
        (w_out_full, w_pw2_full, queries, fresh)
    )
    w_pw2_cols = lax.dynamic_slice_in_dim(w_pw2_full, me * local_width, local_width, 1).reshape(
        groups, local_width, local_width
    )

    got_mover = frame_got[:, out_span + 1 + conv_len, 0].astype(jnp.int32)
    movers = jnp.arange(moving, dtype=jnp.int32)
    mover_from = (movers[:, None] + 1 == got_mover[None, :]).astype(jnp.bfloat16)
    moved_kv = jnp.einsum(
        "jo,orc->jrc", mover_from, cache_got[:, :kv_rows], preferred_element_type=jnp.float32
    ).astype(jnp.bfloat16)
    moved_conv = jnp.einsum(
        "jo,orc->jrc",
        mover_from,
        frame_got[:, out_span + 1 : out_span + 1 + conv_len],
        preferred_element_type=jnp.float32,
    ).astype(jnp.bfloat16)
    kv_state = jnp.concatenate(
        [kv_cache[:settled, 0], moved_kv.reshape(moving, cache_len, kv_lanes)], axis=0
    )
    conv_state = jnp.concatenate([conv_cache[:settled], moved_conv], axis=0)

    memory = jnp.concatenate([kv_state, fresh], axis=1)
    keys_total = memory.shape[1]
    scores = jnp.einsum(
        "sqd,skd->sqk", queries, memory[..., :head_dim], preferred_element_type=jnp.float32
    ) * head_dim ** (-0.5)
    frame_index = jnp.arange(frame_span, dtype=jnp.int32)
    block_of = frame_index // horizon
    low = block_of * horizon
    high = cache_len + jnp.minimum(frames[:, None], (block_of[None, :] + 1) * horizon)
    position = jnp.arange(keys_total, dtype=jnp.int32)
    live_keys = (position[None, None, :] >= low[None, :, None]) & (
        position[None, None, :] < high[:, :, None]
    )
    scores = jnp.where(live_keys, scores, -1e30)
    row_max = jnp.max(scores, axis=-1, keepdims=True)
    weights = jnp.exp(scores - row_max)
    probabilities = (weights / jnp.sum(weights, axis=-1, keepdims=True)).astype(jnp.bfloat16)
    context = jnp.einsum(
        "sqk,skd->sqd", probabilities, memory[..., head_dim:], preferred_element_type=jnp.float32
    ).astype(jnp.bfloat16)

    ctx_all = lax.all_gather(context, "ingest", axis=0, tiled=False)
    row_count = utterances * frame_span
    attn = jnp.einsum(
        "grc,gcn->rn",
        ctx_all.reshape(groups, row_count, head_dim),
        w_out_full.reshape(groups, head_dim, model_width),
        preferred_element_type=jnp.float32,
    )
    residual = x_rows.reshape(row_count, model_width) + attn
    normed2 = normalize(residual, ln2_gain)
    mixed = jnp.dot(
        normed2, w_pw1.reshape(model_width, 2 * local_width), preferred_element_type=jnp.float32
    )
    glu_out = (mixed[:, :local_width] * jax.nn.sigmoid(mixed[:, local_width:])).astype(
        jnp.bfloat16
    )
    glu_out = glu_out.reshape(utterances, frame_span, local_width)

    joined = jnp.concatenate([conv_state, glu_out], axis=1)
    joined_f = joined.astype(jnp.float32)
    running = jnp.zeros((utterances, frame_span, local_width), jnp.float32)
    for tap_index in range(taps):
        running = running + joined_f[:, tap_index : tap_index + frame_span, :] * dw_weight[
            tap_index
        ].astype(jnp.float32)
    activated = jax.nn.silu(running * bn_scale + bn_shift).astype(jnp.bfloat16)

    act_all = lax.all_gather(activated, "ingest", axis=0, tiled=False)
    conv_terms = jnp.einsum(
        "grc,gcn->rn",
        act_all.reshape(groups, row_count, local_width),
        w_pw2_cols,
        preferred_element_type=jnp.float32,
    )
    residual_own = lax.dynamic_slice_in_dim(residual, me * local_width, local_width, 1)
    result = (residual_own + conv_terms).reshape(utterances, frame_span, local_width)
    live_rows = frame_index[None, :] < frames[:, None]
    layer_out = jnp.where(live_rows[:, :, None], result, 0.0).astype(jnp.bfloat16)
    layer_out = layer_out[:, :out_span]

    keep = jnp.arange(cache_len, dtype=jnp.int32)
    kv_pick = position[None, None, :] == keep[None, :, None] + frames[:, None, None]
    kv_next = jnp.einsum(
        "srp,spd->srd", kv_pick.astype(jnp.bfloat16), memory, preferred_element_type=jnp.float32
    ).astype(jnp.bfloat16)
    conv_keep = jnp.arange(conv_len, dtype=jnp.int32)
    conv_pos = jnp.arange(joined.shape[1], dtype=jnp.int32)
    conv_pick = conv_pos[None, None, :] == conv_keep[None, :, None] + frames[:, None, None]
    conv_next = jnp.einsum(
        "srp,spd->srd", conv_pick.astype(jnp.bfloat16), joined, preferred_element_type=jnp.float32
    ).astype(jnp.bfloat16)
    return (layer_out, kv_next.reshape(kv_cache.shape), conv_next)


def solution(mesh):
    in_specs = (
        P("owner", None, "ingest"),
        P("owner"),
        P("owner"),
        P("owner"),
        P("owner", "ingest", None, None),
        P("owner", None, "ingest"),
        P("owner"),
        P(),
        P(None, "ingest", None),
        P("ingest", None),
        P(),
        P(None, None, "ingest"),
        P(None, "ingest"),
        P("ingest"),
        P("ingest"),
        P("ingest", None),
    )
    out_specs = (
        P("owner", None, "ingest"),
        P("owner", "ingest", None, None),
        P("owner", None, "ingest"),
    )
    return jax.shard_map(shards, mesh=mesh, in_specs=in_specs, out_specs=out_specs, check_vma=False)
```
